32 devices in a mesh: band: 4 (over z), lon: 8 (over y, x, core).
Axes of the slice: x: 2, y: 2, z: 4, core: 2. Of those that a mesh axis runs over, the one named last changes fastest.
Arguments:
- control: float32 [50, 128, 1024], P(None, 'band', 'lon'), may hold values from -6 to 6
- background_std: float32 [50], replicated, may hold values from 0.5 to 2
- diffusivity: float32 [128, 1024], P('band', 'lon'), may hold values from 0.03 to 0.24
- land_sea: int32 [128, 1024], P('band', 'lon'), may hold values 0 or 1
- departures: float32 [50, 131072], P(None, ('band', 'lon')), may hold values from -6 to 6
- obs_frac: float32 [2, 131072], P(None, ('band', 'lon')), may hold values from 0 to 1
- obs_weight: float32 [131072], P(('band', 'lon')), may hold values from 0.2 to 2
- obs_cell: int32 [131072], P(('band', 'lon')), may hold values from 0 to 3936
- obs_tile: int32 [131072, 1], P(('band', 'lon')), may hold values from 0 to 31; in each aligned block of 4096 rows (0 to 4095, 4096 to 8191, ...) at most 160 rows name the same one
Outputs:
- gradient: float32 [50, 128, 1024], P(None, 'band', 'lon')
- obs_residual: float32 [50, 131072], P(None, ('band', 'lon'))
The draws below stay inside these ranges and needn't reach their ends.
Inputs may be any that keep to these rules, and one draw needn't show every extreme that they name: `obs_tile`: in the rows of one device at most 160 name the same tile, a bound that some block reaches of them.
All inputs are finite; a program needn't handle non-finite values. No bound on the sum of `land_sea` on one device may be relied on, other than what follows from the above.
Results may differ from the reference program's by a relative error of at most 0.0003.
Values sent between devices are 32-bit elements; how exact they have to be, the bound alone decides.
No kernel may reach another device: no remote copies, remote signals or barrier semaphores. Data moves between devices by JAX's collectives and lax.ppermute only.
A program may use at most 128 MiB of HBM per device.

```python
import math
import jax
import jax.numpy as jnp
import numpy as np
from jax import lax

VALS = 50
CLAT = 32
CLON = 128
OBS_DEV = 4096
PASSES = 4
CAP = 160
NLAT = 128
NLON = 1024
OBS_TOTAL = 131072
N_LON = 8
DEVICES = 32


def place_ends(drawn, rng, smallest, high):
    place = [jax.random.randint(jax.random.fold_in(rng, axis), (), 0, length) for axis, length in enumerate(drawn.shape)]
    longest = drawn.shape.index(max(drawn.shape))
    beside = place[:longest] + [(place[longest] + 1) % drawn.shape[longest]] + place[longest + 1:]
    return drawn.at[tuple(place)].set(smallest).at[tuple(beside)].set(high)


def shard_levels(own_key, shape, split, least, high):
    def one(axis_at, blocks):
        draws = jax.random.uniform(jax.random.fold_in(jax.random.fold_in(own_key, 6), axis_at), (blocks,), jnp.float32, least / len(split), high / len(split))
        return jnp.repeat(jnp.exp(draws), shape[axis_at] // blocks).reshape((-1,) + (1,) * (len(shape) - axis_at - 1))

    gain = one(*split[0])
    for cut in split[1:]:
        gain = gain * one(*cut)
    return gain


def routed_block(stream_key, own, number, rows, number_of, top, bound, slope):
    sequence = jax.random.permutation(stream_key, number_of)
    crowded, usual = portions_of(number_of, rows * top, bound, slope, True), portions_of(number_of, rows * top, bound, slope, False)
    places = jnp.arange(number_of)

    def named(tallies, turn):
        used = int((tallies > 0).sum())
        fixed = max(1, used // 4)
        moved = fixed + (places - fixed + turn * (used - fixed)) % max(1, number_of - fixed)
        return jnp.zeros((number_of,), jnp.int32).at[sequence[jnp.where(places < fixed, places, moved)]].set(jnp.asarray(tallies, jnp.int32))

    tallies = jnp.where(number % 4 == 0, named(crowded, number // 4), named(usual, number - number // 4 - 1))
    mixed = jax.random.permutation(jax.random.fold_in(own, 3), number_of)
    giver, receiver = mixed[0:number_of // 2 * 2:2], mixed[1:number_of // 2 * 2:2]
    slack = jnp.minimum(tallies[giver] - 1, bound - tallies[receiver]) // 2
    slack = jnp.where((giver == sequence[0]) | (receiver == sequence[0]) | (tallies[receiver] == 0), 0, jnp.maximum(slack, 0))
    moved = jax.random.randint(jax.random.fold_in(own, 4), (number_of // 2,), 0, 1 << 20) % (slack + 1)
    tallies = tallies.at[giver].add(-moved).at[receiver].add(moved)
    items = jnp.searchsorted(jnp.cumsum(tallies), jnp.arange(rows * top), side="right").astype(jnp.int32)
    listing = items.reshape(top, rows).T
    listing = listing[jax.random.permutation(jax.random.fold_in(own, 1), rows)]
    turn = jax.random.randint(jax.random.fold_in(own, 2), (rows, 1), 0, top)
    return jnp.take_along_axis(listing, (jnp.arange(top)[None, :] + turn) % top, axis=1)


def portions_of(number_of, total, bound, skew, full):
    weights = [(1 << 20) // math.isqrt(grade ** skew) + 1 for grade in range(1, number_of + 1)]
    largest = bound if full else min(bound, max(-(-total // number_of), total * weights[0] // sum(weights)))
    least = 1 if total - largest >= number_of - 1 else 0
    counts, rest = [largest] + [least] * (number_of - 1), total - largest - least * (number_of - 1)
    while rest > 0:
        movable = [i for i in range(1, number_of) if counts[i] < largest] or [i for i in range(1, number_of) if counts[i] < bound]
        mass, left = sum([weights[i] for i in movable]), rest
        for i in movable:
            addition = min(bound - counts[i], max(1, left * weights[i] // mass), rest)
            counts[i] = counts[i] + addition
            rest = rest - addition
    return np.array(counts)


def bell_draw(stream_key, extent, scale, reach, cuts=(), dtype=jnp.bfloat16):
    result = scale * jax.random.normal(stream_key, extent, jnp.float32)
    if cuts:
        result = result * shard_levels(stream_key, extent, cuts, -0.22, 0.18)
    return jnp.clip(result, -reach, reach).astype(dtype)


def setup_inputs(seed: int = 0) -> dict:
    splits = jax.random.split(jax.random.key(seed), 10)
    control = bell_draw(splits[0], (VALS, NLAT, NLON), 1.0, 6.0, ((1, 4), (2, 8)), jnp.float32)
    background_std = jnp.clip(jnp.exp(jax.random.uniform(splits[1], (VALS,), jnp.float32, math.log(0.5), math.log(2.0))), 0.5, 2.0)
    diffusivity = jnp.clip(jnp.exp(math.log(0.24) - 2.0794415 * jax.random.uniform(splits[2], (NLAT, NLON), jnp.float32) ** shard_levels(splits[2], (NLAT, NLON), ((0, 4), (1, 8)), -0.2, 0.2)), 0.03, 0.24)
    land_sea = place_ends((jax.random.randint(splits[3], (NLAT, NLON), 0, 10) < 7).astype(jnp.int32), jax.random.fold_in(splits[3], 1), 0, 1)
    departures = bell_draw(splits[4], (VALS, OBS_TOTAL), 1.0, 6.0, ((1, 32),), jnp.float32)
    obs_frac = jnp.clip(1.0 * jax.random.uniform(splits[5], (2, OBS_TOTAL), jnp.float32) ** shard_levels(splits[5], (2, OBS_TOTAL), ((1, 32),), -0.2, 0.2), 0.0, 1.0)
    obs_weight = jnp.clip(jnp.exp(math.log(2.0) - 2.3025851 * jax.random.uniform(splits[6], (OBS_TOTAL,), jnp.float32) ** shard_levels(splits[6], (OBS_TOTAL,), ((0, 32),), -0.2, 0.2)), 0.2, 2.0)
    obs_cell = place_ends(jax.random.randint(splits[7], (OBS_TOTAL,), 0, (CLAT - 1) * (CLON - 1)), jax.random.fold_in(splits[7], 1), 0, ((CLAT - 1) * (CLON - 1)) - 1).astype(jnp.int32)
    obs_tile_keys = jax.random.split(jax.random.fold_in(splits[8], 1), OBS_TOTAL // OBS_DEV)
    obs_tile_turns = jax.random.permutation(jax.random.fold_in(splits[8], 3), OBS_TOTAL // OBS_DEV)
    obs_tile = jax.vmap(lambda own, number: routed_block(jax.random.fold_in(splits[8], 2), own, number, OBS_DEV, DEVICES, 1, CAP, 2))(obs_tile_keys, obs_tile_turns).reshape((OBS_TOTAL, 1))
    return dict(control=control, background_std=background_std, diffusivity=diffusivity, land_sea=land_sea, departures=departures, obs_frac=obs_frac, obs_weight=obs_weight, obs_cell=obs_cell, obs_tile=obs_tile)


def face_weights(diffusivity, sea):
    south = 0.5 * (diffusivity[:-1, :] + diffusivity[1:, :]) * sea[:-1, :] * sea[1:, :]
    rolled_kappa = jnp.roll(diffusivity, -1, axis=1)
    rolled_sea = jnp.roll(sea, -1, axis=1)
    east = 0.5 * (diffusivity + rolled_kappa) * sea * rolled_sea
    return south, east


def operate(field, south, east):
    flux_south = south * (field[:, 1:, :] - field[:, :-1, :])
    border = jnp.zeros((field.shape[0], 1, field.shape[2]), jnp.float32)
    along_lat = jnp.concatenate([flux_south, border], axis=1) - jnp.concatenate([border, flux_south], axis=1)
    flux_east = east * (jnp.roll(field, -1, axis=2) - field)
    along_lon = flux_east - jnp.roll(flux_east, 1, axis=2)
    return field + along_lat + along_lon


def reference(control, background_std, diffusivity, land_sea, departures, obs_frac, obs_weight, obs_cell, obs_tile):
    sea = land_sea.astype(jnp.float32)
    south, east = face_weights(diffusivity, sea)
    state = control * sea[None]
    for step in range(PASSES):
        state = operate(state, south, east)
    increment = state * background_std[:, None, None]
    tiles = obs_tile[:, 0]
    band_row = tiles // N_LON
    lon_col = tiles % N_LON
    lat_index = band_row * CLAT + obs_cell // (CLON - 1)
    lon_index = lon_col * CLON + obs_cell % (CLON - 1)
    base = (lat_index * NLON + lon_index).astype(jnp.int32)
    corners = (base, base + NLON, base + 1, base + NLON + 1)
    lat_frac = obs_frac[0]
    lon_frac = obs_frac[1]
    weights = ((1.0 - lat_frac) * (1.0 - lon_frac), lat_frac * (1.0 - lon_frac),
               (1.0 - lat_frac) * lon_frac, lat_frac * lon_frac)
    flat = increment.reshape(VALS, NLAT * NLON)

    def forward_level(pair):
        level, depart = pair
        equiv = weights[0] * level[corners[0]] + weights[1] * level[corners[1]]
        equiv = equiv + weights[2] * level[corners[2]] + weights[3] * level[corners[3]]
        return obs_weight * (equiv - depart)

    residual = lax.map(forward_level, (flat, departures))

    def adjoint_level(level_resid):
        cells = jnp.zeros((NLAT * NLON,), jnp.float32)
        for corner, weight in zip(corners, weights):
            cells = cells.at[corner].add(weight * level_resid)
        return cells

    adjoint = lax.map(adjoint_level, residual).reshape(VALS, NLAT, NLON)
    state = adjoint * background_std[:, None, None]
    for step in range(PASSES):
        state = operate(state, south, east)
    gradient = control + sea[None] * state
    return gradient, residual
```

```python
import jax
import jax.numpy as jnp
from jax import lax
from jax.sharding import PartitionSpec as P

PASSES = 4


HIGH = lax.Precision.HIGH


def ring_halo(array, axis, dim, width):
    count, length = (lax.axis_size(axis), array.shape[dim])
    up = [(i, (i + 1) % count) for i in range(count)]
    down = [(j, i) for i, j in up]
    last = lax.slice_in_dim(array, length - width, length, axis=dim)
    initial = lax.slice_in_dim(array, 0, width, axis=dim)
    before = lax.ppermute(last, axis, up)
    after = lax.ppermute(initial, axis, down)
    return jnp.concatenate([before, array, after], axis=dim)


def with_halo(array, width):
    array = ring_halo(array, "band", array.ndim - 2, width)
    return ring_halo(array, "lon", array.ndim - 1, width)


def face_weights(kappa_pad, sea_pad):
    south = 0.5 * (kappa_pad[:-1, :] + kappa_pad[1:, :]) * sea_pad[:-1, :] * sea_pad[1:, :]
    east = 0.5 * (kappa_pad[:, :-1] + kappa_pad[:, 1:]) * sea_pad[:, :-1] * sea_pad[:, 1:]
    return (south, east)


def diffuse_once(field, south, east):
    flux_south = south * (field[:, 1:, :] - field[:, :-1, :])
    flux_east = east * (field[:, :, 1:] - field[:, :, :-1])
    zero_lat = ((0, 0), (0, 1), (0, 0))
    along_lat = jnp.pad(flux_south, zero_lat) - jnp.pad(flux_south, ((0, 0), (1, 0), (0, 0)))
    along_lon = jnp.pad(flux_east, ((0, 0), (0, 0), (0, 1))) - jnp.pad(flux_east, ((0, 0), (0, 0), (1, 0)))
    return field + along_lat + along_lon


def smooth(field, south, east):
    tile_lat, tile_lon = field.shape[1], field.shape[2]
    result = with_halo(field, PASSES)
    for step in range(PASSES):
        result = diffuse_once(result, south, east)
    return result[:, PASSES:PASSES + tile_lat, PASSES:PASSES + tile_lon]


def split3(x):
    hi = lax.reduce_precision(x, exponent_bits=8, mantissa_bits=7)
    rest = x - hi
    mid = lax.reduce_precision(rest, exponent_bits=8, mantissa_bits=7)
    lo = rest - mid
    parts = [part.astype(jnp.bfloat16) for part in (hi, mid, lo)]
    return jnp.concatenate(parts, axis=0)


def join3(parts):
    rows = parts.shape[0] // 3
    return (parts[:rows] + parts[rows:2 * rows]) + parts[2 * rows:]


def slot_of(tiles, devices, block_rows):
    count = tiles.shape[0]
    blocks = count // block_rows
    one_hot = (tiles[:, None] == jnp.arange(devices, dtype=jnp.int32)[None, :]).astype(jnp.bfloat16)
    one_hot = one_hot.reshape(blocks, block_rows, devices)
    positions = jnp.arange(block_rows, dtype=jnp.int32)
    lower_tri = (positions[:, None] > positions[None, :]).astype(jnp.bfloat16)
    within = jnp.einsum("ab,kbt->kat", lower_tri, one_hot, preferred_element_type=jnp.float32)
    totals = jnp.sum(one_hot.astype(jnp.float32), axis=1)
    offsets = jnp.cumsum(totals, axis=0) - totals
    before = within + offsets[:, None, :]
    rank = jnp.sum(before * one_hot.astype(jnp.float32), axis=2)
    return rank.reshape(count).astype(jnp.int32)


def on_device(
    control,
    background_std,
    diffusivity,
    land_sea,
    departures,
    obs_frac,
    obs_weight,
    obs_cell,
    obs_tile,
):
    values = control.shape[0]
    tile_lat = control.shape[1]
    tile_lon = control.shape[2]
    band_count = lax.axis_size("band")
    lon_count = lax.axis_size("lon")
    devices = band_count * lon_count
    sea = land_sea.astype(jnp.float32)
    stacked = jnp.stack([diffusivity, sea])
    depth = PASSES
    rimmed = with_halo(stacked, depth)
    lat_rows = (
        lax.axis_index("band") * tile_lat
        - depth
        + jnp.arange(tile_lat + 2 * depth, dtype=jnp.int32)
    )
    inside = ((lat_rows >= 0) & (lat_rows < band_count * tile_lat)).astype(jnp.float32)
    south, east = face_weights(rimmed[0], rimmed[1] * inside[:, None])
    state = smooth(control * sea[None], south, east)
    increment = state * background_std[:, None, None]
    count = obs_tile.shape[0]
    block_rows = 512
    blocks = count // block_rows
    capacity = 5 * count // (4 * devices)
    slots = devices * capacity
    tiles = obs_tile[:, 0]
    target = tiles * capacity + slot_of(tiles, devices, block_rows)
    target_blocks = target.reshape(blocks, block_rows)
    slot_ids = jnp.arange(slots, dtype=jnp.int32)
    payload = jnp.concatenate(
        [departures, obs_frac, obs_weight[None, :], obs_cell.astype(jnp.float32)[None, :]], axis=0
    )
    payload_blocks = split3(payload).reshape(3 * (values + 4), blocks, block_rows)

    def place_block(index, total):
        select = (target_blocks[index][:, None] == slot_ids[None, :]).astype(jnp.bfloat16)
        piece = payload_blocks[:, index, :]
        return total + jnp.dot(piece, select, preferred_element_type=jnp.float32)

    outgoing = lax.fori_loop(0, blocks, place_block, jnp.zeros((3 * (values + 4), slots), jnp.float32))
    outgoing = join3(outgoing)
    arrived = lax.all_to_all(
        outgoing.reshape(values + 4, devices, capacity),
        ("band", "lon"),
        split_axis=1,
        concat_axis=1,
        tiled=True,
    )
    arrived = arrived.reshape(values + 4, slots)
    depart = arrived[:values]
    lat_frac = arrived[values]
    lon_frac = arrived[values + 1]
    row_weight = arrived[values + 2]
    cell = arrived[values + 3].astype(jnp.int32)
    lat_start = cell // (tile_lon - 1)
    lon_start = cell % (tile_lon - 1)
    lat_ids = jnp.arange(tile_lat, dtype=jnp.int32)[:, None]
    lon_ids = jnp.arange(tile_lon, dtype=jnp.int32)[:, None]
    lat_table = (lat_ids == lat_start[None, :]).astype(jnp.float32) * (1.0 - lat_frac)[None, :]
    lat_table = (
        lat_table + (lat_ids == lat_start[None, :] + 1).astype(jnp.float32) * lat_frac[None, :]
    )
    lon_table = (lon_ids == lon_start[None, :]).astype(jnp.float32) * (1.0 - lon_frac)[None, :]
    lon_table = (
        lon_table + (lon_ids == lon_start[None, :] + 1).astype(jnp.float32) * lon_frac[None, :]
    )
    partial_rows = jnp.einsum(
        "vij,jn->vin", increment, lon_table, precision=HIGH, preferred_element_type=jnp.float32
    )
    equiv = jnp.sum(partial_rows * lat_table[None, :, :], axis=1)
    misfit = row_weight * (equiv - depart)
    spread = misfit[:, None, :] * lat_table[None, :, :]
    adjoint = jnp.einsum(
        "vin,jn->vij", spread, lon_table, precision=HIGH, preferred_element_type=jnp.float32
    )
    adjoint = adjoint * background_std[:, None, None]
    gradient = control + sea[None] * smooth(adjoint, south, east)
    returned = lax.all_to_all(
        misfit.reshape(values, devices, capacity),
        ("band", "lon"),
        split_axis=1,
        concat_axis=1,
        tiled=True,
    )
    returned = split3(returned.reshape(values, slots))

    def pick_block(block_target):
        select = (slot_ids[:, None] == block_target[None, :]).astype(jnp.bfloat16)
        return join3(jnp.dot(returned, select, preferred_element_type=jnp.float32))

    picked = lax.map(pick_block, target_blocks)
    obs_residual = jnp.transpose(picked, (1, 0, 2)).reshape(values, count)
    return (gradient, obs_residual)


def solution(mesh):
    in_specs = (
        P(None, "band", "lon"),
        P(),
        P("band", "lon"),
        P("band", "lon"),
        P(None, ("band", "lon")),
        P(None, ("band", "lon")),
        P(("band", "lon")),
        P(("band", "lon")),
        P(("band", "lon"), None),
    )
    out_specs = (P(None, "band", "lon"), P(None, ("band", "lon")))
    return jax.shard_map(
        on_device, mesh=mesh, in_specs=in_specs, out_specs=out_specs, check_vma=False
    )
```

```python
import jax
import jax.numpy as jnp
from jax import lax
from jax.experimental import pallas as pl
from jax.experimental.pallas import tpu as pltpu
from jax.sharding import PartitionSpec as P

PASSES = 4


HIGH = lax.Precision.HIGH


def ring_halo(array, axis, dim, width):
    count, length = (lax.axis_size(axis), array.shape[dim])
    up = [(i, (i + 1) % count) for i in range(count)]
    down = [(j, i) for i, j in up]
    last = lax.slice_in_dim(array, length - width, length, axis=dim)
    initial = lax.slice_in_dim(array, 0, width, axis=dim)
    before = lax.ppermute(last, axis, up)
    after = lax.ppermute(initial, axis, down)
    return jnp.concatenate([before, array, after], axis=dim)


def with_halo(array, width):
    array = ring_halo(array, "band", array.ndim - 2, width)
    return ring_halo(array, "lon", array.ndim - 1, width)


def face_weights(kappa_pad, sea_pad):
    south = 0.5 * (kappa_pad[:-1, :] + kappa_pad[1:, :]) * sea_pad[:-1, :] * sea_pad[1:, :]
    east = 0.5 * (kappa_pad[:, :-1] + kappa_pad[:, 1:]) * sea_pad[:, :-1] * sea_pad[:, 1:]
    return (south, east)


def diffuse_once(field, south, east):
    flux_south = south * (field[:, 1:, :] - field[:, :-1, :])
    flux_east = east * (field[:, :, 1:] - field[:, :, :-1])
    zero_lat = ((0, 0), (0, 1), (0, 0))
    along_lat = jnp.pad(flux_south, zero_lat) - jnp.pad(flux_south, ((0, 0), (1, 0), (0, 0)))
    along_lon = jnp.pad(flux_east, ((0, 0), (0, 0), (0, 1))) - jnp.pad(flux_east, ((0, 0), (0, 0), (1, 0)))
    return field + along_lat + along_lon


def smooth(field, south, east):
    tile_lat, tile_lon = field.shape[1], field.shape[2]
    result = with_halo(field, PASSES)
    for step in range(PASSES):
        result = diffuse_once(result, south, east)
    return result[:, PASSES:PASSES + tile_lat, PASSES:PASSES + tile_lon]


def scatter_kernel(target_ref, rows_ref, out_ref):
    out_ref[...] = jnp.zeros(out_ref.shape, out_ref.dtype)

    def body(n, carry):
        out_ref[pl.ds(target_ref[n], 1), :] = rows_ref[pl.ds(n, 1), :]
        return carry

    lax.fori_loop(0, rows_ref.shape[0], body, 0, unroll=8)


def gather_kernel(source_ref, rows_ref, out_ref):
    def body(n, carry):
        out_ref[pl.ds(n, 1), :] = rows_ref[pl.ds(source_ref[n], 1), :]
        return carry

    lax.fori_loop(0, out_ref.shape[0], body, 0, unroll=8)


def scatter_rows(target, rows, slots):
    return pl.pallas_call(
        scatter_kernel,
        out_shape=jax.ShapeDtypeStruct((slots, rows.shape[1]), rows.dtype),
        in_specs=[pl.BlockSpec(memory_space=pltpu.SMEM), pl.BlockSpec(memory_space=pltpu.VMEM)],
        out_specs=pl.BlockSpec(memory_space=pltpu.VMEM),
    )(target, rows)


def gather_rows(source, rows):
    return pl.pallas_call(
        gather_kernel,
        out_shape=jax.ShapeDtypeStruct((source.shape[0], rows.shape[1]), rows.dtype),
        in_specs=[pl.BlockSpec(memory_space=pltpu.SMEM), pl.BlockSpec(memory_space=pltpu.VMEM)],
        out_specs=pl.BlockSpec(memory_space=pltpu.VMEM),
    )(source, rows)


def exchange_rows(rows, devices):
    slots, width = rows.shape
    chunk = slots // devices * width
    padded = -(-chunk // 1024) * 1024
    flat = jnp.pad(rows.reshape(devices, chunk), ((0, 0), (0, padded - chunk)))
    arrived = lax.all_to_all(
        flat.reshape(devices, padded // 128, 128), ("band", "lon"), 0, 0, tiled=True
    )
    return arrived.reshape(devices, padded)[:, :chunk].reshape(slots, width)


def slot_of(tiles, devices, block_rows):
    count = tiles.shape[0]
    blocks = count // block_rows
    one_hot = (tiles[:, None] == jnp.arange(devices, dtype=jnp.int32)[None, :]).astype(jnp.bfloat16)
    one_hot = one_hot.reshape(blocks, block_rows, devices)
    positions = jnp.arange(block_rows, dtype=jnp.int32)
    lower_tri = (positions[:, None] > positions[None, :]).astype(jnp.bfloat16)
    within = jnp.einsum("ab,kbt->kat", lower_tri, one_hot, preferred_element_type=jnp.float32)
    totals = jnp.sum(one_hot.astype(jnp.float32), axis=1)
    offsets = jnp.cumsum(totals, axis=0) - totals
    before = within + offsets[:, None, :]
    rank = jnp.sum(before * one_hot.astype(jnp.float32), axis=2)
    return rank.reshape(count).astype(jnp.int32)


def on_device(
    control,
    background_std,
    diffusivity,
    land_sea,
    departures,
    obs_frac,
    obs_weight,
    obs_cell,
    obs_tile,
):
    values = control.shape[0]
    tile_lat = control.shape[1]
    tile_lon = control.shape[2]
    band_count = lax.axis_size("band")
    lon_count = lax.axis_size("lon")
    devices = band_count * lon_count
    sea = land_sea.astype(jnp.float32)
    stacked = jnp.stack([diffusivity, sea])
    depth = PASSES
    rimmed = with_halo(stacked, depth)
    lat_rows = (
        lax.axis_index("band") * tile_lat
        - depth
        + jnp.arange(tile_lat + 2 * depth, dtype=jnp.int32)
    )
    inside = ((lat_rows >= 0) & (lat_rows < band_count * tile_lat)).astype(jnp.float32)
    south, east = face_weights(rimmed[0], rimmed[1] * inside[:, None])
    state = smooth(control * sea[None], south, east)
    increment = state * background_std[:, None, None]
    count = obs_tile.shape[0]
    block_rows = 512
    blocks = count // block_rows
    capacity = 5 * count // (4 * devices)
    slots = devices * capacity
    tiles = obs_tile[:, 0]
    target = tiles * capacity + slot_of(tiles, devices, block_rows)
    target = jnp.clip(target, 0, slots - 1)
    payload = jnp.concatenate(
        [departures, obs_frac, obs_weight[None, :], obs_cell.astype(jnp.float32)[None, :]], axis=0
    )
    outgoing = scatter_rows(target, payload.T, slots)
    arrived = exchange_rows(outgoing, devices).T
    depart = arrived[:values]
    lat_frac = arrived[values]
    lon_frac = arrived[values + 1]
    row_weight = arrived[values + 2]
    cell = arrived[values + 3].astype(jnp.int32)
    lat_start = cell // (tile_lon - 1)
    lon_start = cell % (tile_lon - 1)
    lat_ids = jnp.arange(tile_lat, dtype=jnp.int32)[:, None]
    lon_ids = jnp.arange(tile_lon, dtype=jnp.int32)[:, None]
    lat_table = (lat_ids == lat_start[None, :]).astype(jnp.float32) * (1.0 - lat_frac)[None, :]
    lat_table = (
        lat_table + (lat_ids == lat_start[None, :] + 1).astype(jnp.float32) * lat_frac[None, :]
    )
    lon_table = (lon_ids == lon_start[None, :]).astype(jnp.float32) * (1.0 - lon_frac)[None, :]
    lon_table = (
        lon_table + (lon_ids == lon_start[None, :] + 1).astype(jnp.float32) * lon_frac[None, :]
    )
    partial_rows = jnp.einsum(
        "vij,jn->vin", increment, lon_table, precision=HIGH, preferred_element_type=jnp.float32
    )
    equiv = jnp.sum(partial_rows * lat_table[None, :, :], axis=1)
    misfit = row_weight * (equiv - depart)
    spread = misfit[:, None, :] * lat_table[None, :, :]
    adjoint = jnp.einsum(
        "vin,jn->vij", spread, lon_table, precision=HIGH, preferred_element_type=jnp.float32
    )
    adjoint = adjoint * background_std[:, None, None]
    gradient = control + sea[None] * smooth(adjoint, south, east)
    returned = exchange_rows(misfit.T, devices)
    obs_residual = gather_rows(target, returned).T
    return (gradient, obs_residual)


def solution(mesh):
    in_specs = (
        P(None, "band", "lon"),
        P(),
        P("band", "lon"),
        P("band", "lon"),
        P(None, ("band", "lon")),
        P(None, ("band", "lon")),
        P(("band", "lon")),
        P(("band", "lon")),
        P(("band", "lon"), None),
    )
    out_specs = (P(None, "band", "lon"), P(None, ("band", "lon")))
    return jax.shard_map(
        on_device, mesh=mesh, in_specs=in_specs, out_specs=out_specs, check_vma=False
    )
```

```python
import jax
import jax.numpy as jnp
from jax import lax
from jax.experimental import pallas as pl
from jax.experimental.pallas import tpu as pltpu
from jax.sharding import PartitionSpec as P

PASSES = 4


HIGH = lax.Precision.HIGH


def ring_halo(array, axis, dim, width):
    count, length = (lax.axis_size(axis), array.shape[dim])
    up = [(i, (i + 1) % count) for i in range(count)]
    down = [(j, i) for i, j in up]
    last = lax.slice_in_dim(array, length - width, length, axis=dim)
    initial = lax.slice_in_dim(array, 0, width, axis=dim)
    before = lax.ppermute(last, axis, up)
    after = lax.ppermute(initial, axis, down)
    return jnp.concatenate([before, array, after], axis=dim)


def with_halo(array, width):
    array = ring_halo(array, "band", array.ndim - 2, width)
    return ring_halo(array, "lon", array.ndim - 1, width)


def face_weights(kappa_pad, sea_pad):
    south = 0.5 * (kappa_pad[:-1, :] + kappa_pad[1:, :]) * sea_pad[:-1, :] * sea_pad[1:, :]
    east = 0.5 * (kappa_pad[:, :-1] + kappa_pad[:, 1:]) * sea_pad[:, :-1] * sea_pad[:, 1:]
    return (south, east)


def diffuse_once(field, south, east):
    flux_south = south * (field[:, 1:, :] - field[:, :-1, :])
    flux_east = east * (field[:, :, 1:] - field[:, :, :-1])
    zero_lat = ((0, 0), (0, 1), (0, 0))
    along_lat = jnp.pad(flux_south, zero_lat) - jnp.pad(flux_south, ((0, 0), (1, 0), (0, 0)))
    along_lon = jnp.pad(flux_east, ((0, 0), (0, 0), (0, 1))) - jnp.pad(flux_east, ((0, 0), (0, 0), (1, 0)))
    return field + along_lat + along_lon


def smooth(field, south, east):
    tile_lat, tile_lon = field.shape[1], field.shape[2]
    result = with_halo(field, PASSES)
    for step in range(PASSES):
        result = diffuse_once(result, south, east)
    return result[:, PASSES:PASSES + tile_lat, PASSES:PASSES + tile_lon]


def scatter_kernel(target_ref, rows_ref, out_ref):
    out_ref[...] = jnp.zeros(out_ref.shape, out_ref.dtype)
    half = out_ref.shape[1] // 2
    left = lax.broadcasted_iota(jnp.int32, (1, out_ref.shape[1]), 1) < half

    def body(n, carry):
        slot = target_ref[n]
        row = pl.ds(slot // 2, 1)
        keep = left == (slot % 2 == 1)
        out_ref[row, :] = jnp.where(keep, out_ref[row, :], rows_ref[pl.ds(n, 1), :])
        return carry

    lax.fori_loop(0, rows_ref.shape[0], body, 0, unroll=8)


def gather_kernel(source_ref, rows_ref, out_ref):
    def body(n, carry):
        out_ref[pl.ds(n, 1), :] = rows_ref[pl.ds(source_ref[n] // 2, 1), :]
        return carry

    lax.fori_loop(0, out_ref.shape[0], body, 0, unroll=8)


def scatter_rows(target, rows, slots):
    return pl.pallas_call(
        scatter_kernel,
        out_shape=jax.ShapeDtypeStruct((slots // 2, rows.shape[1]), rows.dtype),
        in_specs=[pl.BlockSpec(memory_space=pltpu.SMEM), pl.BlockSpec(memory_space=pltpu.VMEM)],
        out_specs=pl.BlockSpec(memory_space=pltpu.VMEM),
    )(target, rows)


def gather_rows(source, rows):
    return pl.pallas_call(
        gather_kernel,
        out_shape=jax.ShapeDtypeStruct((source.shape[0], rows.shape[1]), rows.dtype),
        in_specs=[pl.BlockSpec(memory_space=pltpu.SMEM), pl.BlockSpec(memory_space=pltpu.VMEM)],
        out_specs=pl.BlockSpec(memory_space=pltpu.VMEM),
    )(source, rows)


def exchange_rows(rows):
    return lax.all_to_all(rows, ("lon", "band"), 0, 0, tiled=True)


def doubled_rows(columns, half):
    rows = jnp.pad(columns.T, ((0, 0), (0, half - columns.shape[0])))
    return jnp.concatenate([rows, rows], axis=1)


def as_columns(rows, half):
    return jnp.concatenate([rows[:, :half].T, rows[:, half:].T], axis=1)


def as_rows(columns, half):
    count = columns.shape[1] // 2
    pad = ((0, 0), (0, half - columns.shape[0]))
    left = jnp.pad(columns[:, :count].T, pad)
    right = jnp.pad(columns[:, count:].T, pad)
    return jnp.concatenate([left, right], axis=1)


def slot_of(tiles, devices, block_rows):
    count = tiles.shape[0]
    blocks = count // block_rows
    one_hot = (tiles[:, None] == jnp.arange(devices, dtype=jnp.int32)[None, :]).astype(jnp.bfloat16)
    one_hot = one_hot.reshape(blocks, block_rows, devices)
    positions = jnp.arange(block_rows, dtype=jnp.int32)
    lower_tri = (positions[:, None] > positions[None, :]).astype(jnp.bfloat16)
    within = jnp.einsum("ab,kbt->kat", lower_tri, one_hot, preferred_element_type=jnp.float32)
    totals = jnp.sum(one_hot.astype(jnp.float32), axis=1)
    offsets = jnp.cumsum(totals, axis=0) - totals
    before = within + offsets[:, None, :]
    rank = jnp.sum(before * one_hot.astype(jnp.float32), axis=2)
    return rank.reshape(count).astype(jnp.int32)


def on_device(
    control,
    background_std,
    diffusivity,
    land_sea,
    departures,
    obs_frac,
    obs_weight,
    obs_cell,
    obs_tile,
):
    values = control.shape[0]
    tile_lat = control.shape[1]
    tile_lon = control.shape[2]
    band_count = lax.axis_size("band")
    lon_count = lax.axis_size("lon")
    devices = band_count * lon_count
    sea = land_sea.astype(jnp.float32)
    stacked = jnp.stack([diffusivity, sea])
    depth = PASSES
    rimmed = with_halo(stacked, depth)
    lat_rows = (
        lax.axis_index("band") * tile_lat
        - depth
        + jnp.arange(tile_lat + 2 * depth, dtype=jnp.int32)
    )
    inside = ((lat_rows >= 0) & (lat_rows < band_count * tile_lat)).astype(jnp.float32)
    south, east = face_weights(rimmed[0], rimmed[1] * inside[:, None])
    state = smooth(control * sea[None], south, east)
    increment = state * background_std[:, None, None]
    count = obs_tile.shape[0]
    block_rows = 512
    blocks = count // block_rows
    capacity = 5 * count // (4 * devices)
    slots = devices * capacity
    tiles = obs_tile[:, 0]
    chunk = (tiles % lon_count) * band_count + tiles // lon_count
    target = chunk * capacity + slot_of(tiles, devices, block_rows)
    target = jnp.clip(target, 0, slots - 1)
    payload = jnp.concatenate(
        [departures, obs_frac, obs_weight[None, :], obs_cell.astype(jnp.float32)[None, :]], axis=0
    )
    half = 64
    outgoing = scatter_rows(target, doubled_rows(payload, half), slots)
    arrived = as_columns(exchange_rows(outgoing), half)
    depart = arrived[:values]
    lat_frac = arrived[values]
    lon_frac = arrived[values + 1]
    row_weight = arrived[values + 2]
    cell = arrived[values + 3].astype(jnp.int32)
    lat_start = cell // (tile_lon - 1)
    lon_start = cell % (tile_lon - 1)
    lat_ids = jnp.arange(tile_lat, dtype=jnp.int32)[:, None]
    lon_ids = jnp.arange(tile_lon, dtype=jnp.int32)[:, None]
    lat_table = (lat_ids == lat_start[None, :]).astype(jnp.float32) * (1.0 - lat_frac)[None, :]
    lat_table = (
        lat_table + (lat_ids == lat_start[None, :] + 1).astype(jnp.float32) * lat_frac[None, :]
    )
    lon_table = (lon_ids == lon_start[None, :]).astype(jnp.float32) * (1.0 - lon_frac)[None, :]
    lon_table = (
        lon_table + (lon_ids == lon_start[None, :] + 1).astype(jnp.float32) * lon_frac[None, :]
    )
    partial_rows = jnp.einsum(
        "vij,jn->vin", increment, lon_table, precision=HIGH, preferred_element_type=jnp.float32
    )
    equiv = jnp.sum(partial_rows * lat_table[None, :, :], axis=1)
    misfit = row_weight * (equiv - depart)
    spread = misfit[:, None, :] * lat_table[None, :, :]
    adjoint = jnp.einsum(
        "vin,jn->vij", spread, lon_table, precision=HIGH, preferred_element_type=jnp.float32
    )
    adjoint = adjoint * background_std[:, None, None]
    gradient = control + sea[None] * smooth(adjoint, south, east)
    returned = gather_rows(target, exchange_rows(as_rows(misfit, half)))
    odd = (target % 2 == 1)[:, None]
    obs_residual = jnp.where(odd, returned[:, half:], returned[:, :half])[:, :values].T
    return (gradient, obs_residual)


def solution(mesh):
    in_specs = (
        P(None, "band", "lon"),
        P(),
        P("band", "lon"),
        P("band", "lon"),
        P(None, ("band", "lon")),
        P(None, ("band", "lon")),
        P(("band", "lon")),
        P(("band", "lon")),
        P(("band", "lon"), None),
    )
    out_specs = (P(None, "band", "lon"), P(None, ("band", "lon")))
    return jax.shard_map(
        on_device, mesh=mesh, in_specs=in_specs, out_specs=out_specs, check_vma=False
    )
```

```python
import jax
import jax.numpy as jnp
from jax import lax
from jax.experimental import pallas as pl
from jax.experimental.pallas import tpu as pltpu
from jax.sharding import PartitionSpec as P

PASSES = 4


HIGH = lax.Precision.HIGH


def ring_halo(array, axis, dim, width):
    count, length = (lax.axis_size(axis), array.shape[dim])
    up = [(i, (i + 1) % count) for i in range(count)]
    down = [(j, i) for i, j in up]
    last = lax.slice_in_dim(array, length - width, length, axis=dim)
    initial = lax.slice_in_dim(array, 0, width, axis=dim)
    before = lax.ppermute(last, axis, up)
    after = lax.ppermute(initial, axis, down)
    return jnp.concatenate([before, array, after], axis=dim)


def with_halo(array, width):
    array = ring_halo(array, "band", array.ndim - 2, width)
    return ring_halo(array, "lon", array.ndim - 1, width)


def face_weights(kappa_pad, sea_pad):
    south = 0.5 * (kappa_pad[:-1, :] + kappa_pad[1:, :]) * sea_pad[:-1, :] * sea_pad[1:, :]
    east = 0.5 * (kappa_pad[:, :-1] + kappa_pad[:, 1:]) * sea_pad[:, :-1] * sea_pad[:, 1:]
    return (south, east)


def diffuse_once(field, south, east):
    flux_south = south * (field[:, 1:, :] - field[:, :-1, :])
    flux_east = east * (field[:, :, 1:] - field[:, :, :-1])
    zero_lat = ((0, 0), (0, 1), (0, 0))
    along_lat = jnp.pad(flux_south, zero_lat) - jnp.pad(flux_south, ((0, 0), (1, 0), (0, 0)))
    along_lon = jnp.pad(flux_east, ((0, 0), (0, 0), (0, 1))) - jnp.pad(flux_east, ((0, 0), (0, 0), (1, 0)))
    return field + along_lat + along_lon


def smooth(field, south, east):
    tile_lat, tile_lon = field.shape[1], field.shape[2]
    result = with_halo(field, PASSES)
    for step in range(PASSES):
        result = diffuse_once(result, south, east)
    return result[:, PASSES:PASSES + tile_lat, PASSES:PASSES + tile_lon]


def scatter_kernel(target_ref, rows_ref, out_ref):
    out_ref[...] = jnp.zeros(out_ref.shape, out_ref.dtype)
    half = out_ref.shape[1] // 2
    left = lax.broadcasted_iota(jnp.int32, (1, out_ref.shape[1]), 1) < half

    def body(n, carry):
        slot = target_ref[n]
        row = pl.ds(slot // 2, 1)
        pltpu.store(out_ref.at[row, :], rows_ref[pl.ds(n, 1), :], mask=left == (slot % 2 == 0))
        return carry

    lax.fori_loop(0, rows_ref.shape[0], body, 0, unroll=8)


def gather_kernel(source_ref, rows_ref, out_ref):
    def body(n, carry):
        out_ref[pl.ds(n, 1), :] = rows_ref[pl.ds(source_ref[n] // 2, 1), :]
        return carry

    lax.fori_loop(0, out_ref.shape[0], body, 0, unroll=8)


def scatter_rows(target, rows, slots):
    return pl.pallas_call(
        scatter_kernel,
        out_shape=jax.ShapeDtypeStruct((slots // 2, rows.shape[1]), rows.dtype),
        in_specs=[pl.BlockSpec(memory_space=pltpu.SMEM), pl.BlockSpec(memory_space=pltpu.VMEM)],
        out_specs=pl.BlockSpec(memory_space=pltpu.VMEM),
    )(target, rows)


def gather_rows(source, rows):
    return pl.pallas_call(
        gather_kernel,
        out_shape=jax.ShapeDtypeStruct((source.shape[0], rows.shape[1]), rows.dtype),
        in_specs=[pl.BlockSpec(memory_space=pltpu.SMEM), pl.BlockSpec(memory_space=pltpu.VMEM)],
        out_specs=pl.BlockSpec(memory_space=pltpu.VMEM),
    )(source, rows)


def exchange_rows(rows):
    return lax.all_to_all(rows, ("band", "lon"), 0, 0, tiled=True)


def doubled_rows(columns, half):
    rows = jnp.pad(columns.T, ((0, 0), (0, half - columns.shape[0])))
    return jnp.concatenate([rows, rows], axis=1)


def as_columns(rows, half):
    return jnp.concatenate([rows[:, :half].T, rows[:, half:].T], axis=1)


def as_rows(columns, half):
    count = columns.shape[1] // 2
    pad = ((0, 0), (0, half - columns.shape[0]))
    left = jnp.pad(columns[:, :count].T, pad)
    right = jnp.pad(columns[:, count:].T, pad)
    return jnp.concatenate([left, right], axis=1)


def slot_of(tiles, devices, block_rows):
    count = tiles.shape[0]
    blocks = count // block_rows
    one_hot = (tiles[:, None] == jnp.arange(devices, dtype=jnp.int32)[None, :]).astype(jnp.bfloat16)
    one_hot = one_hot.reshape(blocks, block_rows, devices)
    positions = jnp.arange(block_rows, dtype=jnp.int32)
    lower_tri = (positions[:, None] > positions[None, :]).astype(jnp.bfloat16)
    within = jnp.einsum("ab,kbt->kat", lower_tri, one_hot, preferred_element_type=jnp.float32)
    totals = jnp.sum(one_hot.astype(jnp.float32), axis=1)
    offsets = jnp.cumsum(totals, axis=0) - totals
    before = within + offsets[:, None, :]
    rank = jnp.sum(before * one_hot.astype(jnp.float32), axis=2)
    return rank.reshape(count).astype(jnp.int32)


def on_device(
    control,
    background_std,
    diffusivity,
    land_sea,
    departures,
    obs_frac,
    obs_weight,
    obs_cell,
    obs_tile,
):
    values = control.shape[0]
    tile_lat = control.shape[1]
    tile_lon = control.shape[2]
    band_count = lax.axis_size("band")
    lon_count = lax.axis_size("lon")
    devices = band_count * lon_count
    sea = land_sea.astype(jnp.float32)
    stacked = jnp.stack([diffusivity, sea])
    depth = PASSES
    rimmed = with_halo(stacked, depth)
    lat_rows = (
        lax.axis_index("band") * tile_lat
        - depth
        + jnp.arange(tile_lat + 2 * depth, dtype=jnp.int32)
    )
    inside = ((lat_rows >= 0) & (lat_rows < band_count * tile_lat)).astype(jnp.float32)
    south, east = face_weights(rimmed[0], rimmed[1] * inside[:, None])
    state = smooth(control * sea[None], south, east)
    increment = state * background_std[:, None, None]
    count = obs_tile.shape[0]
    block_rows = 512
    blocks = count // block_rows
    capacity = 5 * count // (4 * devices)
    slots = devices * capacity
    tiles = obs_tile[:, 0]
    target = tiles * capacity + slot_of(tiles, devices, block_rows)
    target = jnp.clip(target, 0, slots - 1)
    payload = jnp.concatenate(
        [departures, obs_frac, obs_weight[None, :], obs_cell.astype(jnp.float32)[None, :]], axis=0
    )
    half = 64
    outgoing = scatter_rows(target, doubled_rows(payload, half), slots)
    arrived = as_columns(exchange_rows(outgoing), half)
    depart = arrived[:values]
    lat_frac = arrived[values]
    lon_frac = arrived[values + 1]
    row_weight = arrived[values + 2]
    cell = arrived[values + 3].astype(jnp.int32)
    lat_start = cell // (tile_lon - 1)
    lon_start = cell % (tile_lon - 1)
    lat_ids = jnp.arange(tile_lat, dtype=jnp.int32)[:, None]
    lon_ids = jnp.arange(tile_lon, dtype=jnp.int32)[:, None]
    lat_table = (lat_ids == lat_start[None, :]).astype(jnp.float32) * (1.0 - lat_frac)[None, :]
    lat_table = (
        lat_table + (lat_ids == lat_start[None, :] + 1).astype(jnp.float32) * lat_frac[None, :]
    )
    lon_table = (lon_ids == lon_start[None, :]).astype(jnp.float32) * (1.0 - lon_frac)[None, :]
    lon_table = (
        lon_table + (lon_ids == lon_start[None, :] + 1).astype(jnp.float32) * lon_frac[None, :]
    )
    partial_rows = jnp.einsum(
        "vij,jn->vin", increment, lon_table, precision=HIGH, preferred_element_type=jnp.float32
    )
    equiv = jnp.sum(partial_rows * lat_table[None, :, :], axis=1)
    misfit = row_weight * (equiv - depart)
    spread = misfit[:, None, :] * lat_table[None, :, :]
    adjoint = jnp.einsum(
        "vin,jn->vij", spread, lon_table, precision=HIGH, preferred_element_type=jnp.float32
    )
    adjoint = adjoint * background_std[:, None, None]
    gradient = control + sea[None] * smooth(adjoint, south, east)
    returned = gather_rows(target, exchange_rows(as_rows(misfit, half)))
    odd = (target % 2 == 1)[:, None]
    obs_residual = jnp.where(odd, returned[:, half:], returned[:, :half])[:, :values].T
    return (gradient, obs_residual)


def solution(mesh):
    in_specs = (
        P(None, "band", "lon"),
        P(),
        P("band", "lon"),
        P("band", "lon"),
        P(None, ("band", "lon")),
        P(None, ("band", "lon")),
        P(("band", "lon")),
        P(("band", "lon")),
        P(("band", "lon"), None),
    )
    out_specs = (P(None, "band", "lon"), P(None, ("band", "lon")))
    return jax.shard_map(
        on_device, mesh=mesh, in_specs=in_specs, out_specs=out_specs, check_vma=False
    )
```

```python
import jax
import jax.numpy as jnp
from jax import lax
from jax.experimental import pallas as pl
from jax.experimental.pallas import tpu as pltpu
from jax.sharding import PartitionSpec as P

PASSES = 4


HIGH = lax.Precision.HIGH


def ring_halo(array, axis, dim, width):
    count, length = (lax.axis_size(axis), array.shape[dim])
    up = [(i, (i + 1) % count) for i in range(count)]
    down = [(j, i) for i, j in up]
    last = lax.slice_in_dim(array, length - width, length, axis=dim)
    initial = lax.slice_in_dim(array, 0, width, axis=dim)
    before = lax.ppermute(last, axis, up)
    after = lax.ppermute(initial, axis, down)
    return jnp.concatenate([before, array, after], axis=dim)


def with_halo(array, width):
    array = ring_halo(array, "band", array.ndim - 2, width)
    return ring_halo(array, "lon", array.ndim - 1, width)


def face_weights(kappa_pad, sea_pad):
    south = 0.5 * (kappa_pad[:-1, :] + kappa_pad[1:, :]) * sea_pad[:-1, :] * sea_pad[1:, :]
    east = 0.5 * (kappa_pad[:, :-1] + kappa_pad[:, 1:]) * sea_pad[:, :-1] * sea_pad[:, 1:]
    return (south, east)


def diffuse_once(field, south, east):
    flux_south = south * (field[:, 1:, :] - field[:, :-1, :])
    flux_east = east * (field[:, :, 1:] - field[:, :, :-1])
    zero_lat = ((0, 0), (0, 1), (0, 0))
    along_lat = jnp.pad(flux_south, zero_lat) - jnp.pad(flux_south, ((0, 0), (1, 0), (0, 0)))
    along_lon = jnp.pad(flux_east, ((0, 0), (0, 0), (0, 1))) - jnp.pad(flux_east, ((0, 0), (0, 0), (1, 0)))
    return field + along_lat + along_lon


def smooth(field, south, east):
    tile_lat, tile_lon = field.shape[1], field.shape[2]
    result = with_halo(field, PASSES)
    for step in range(PASSES):
        result = diffuse_once(result, south, east)
    return result[:, PASSES:PASSES + tile_lat, PASSES:PASSES + tile_lon]


def scatter_kernel(row_ref, odd_ref, rows_ref, out_ref):
    out_ref[...] = jnp.zeros(out_ref.shape, out_ref.dtype)
    half = out_ref.shape[1] // 2
    left = lax.broadcasted_iota(jnp.int32, (1, out_ref.shape[1]), 1) < half

    def body(n, carry):
        mask = left == (odd_ref[n] == 0)
        pltpu.store(out_ref.at[pl.ds(row_ref[n], 1), :], rows_ref[pl.ds(n, 1), :], mask=mask)
        return carry

    lax.fori_loop(0, rows_ref.shape[0], body, 0, unroll=8)


def gather_kernel(source_ref, rows_ref, out_ref):
    def body(n, carry):
        out_ref[pl.ds(n, 1), :] = rows_ref[pl.ds(source_ref[n], 1), :]
        return carry

    lax.fori_loop(0, out_ref.shape[0], body, 0, unroll=8)


def scatter_rows(target, rows, slots):
    smem = pl.BlockSpec(memory_space=pltpu.SMEM)
    return pl.pallas_call(
        scatter_kernel,
        out_shape=jax.ShapeDtypeStruct((slots // 2, rows.shape[1]), rows.dtype),
        in_specs=[smem, smem, pl.BlockSpec(memory_space=pltpu.VMEM)],
        out_specs=pl.BlockSpec(memory_space=pltpu.VMEM),
    )(target // 2, target % 2, rows)


def gather_rows(source, rows):
    return pl.pallas_call(
        gather_kernel,
        out_shape=jax.ShapeDtypeStruct((source.shape[0], rows.shape[1]), rows.dtype),
        in_specs=[pl.BlockSpec(memory_space=pltpu.SMEM), pl.BlockSpec(memory_space=pltpu.VMEM)],
        out_specs=pl.BlockSpec(memory_space=pltpu.VMEM),
    )(source, rows)


def exchange_rows(rows):
    return lax.all_to_all(rows, ("band", "lon"), 0, 0, tiled=True)


def doubled_rows(columns, half):
    rows = jnp.pad(columns.T, ((0, 0), (0, half - columns.shape[0])))
    return jnp.concatenate([rows, rows], axis=1)


def as_columns(rows, half):
    return jnp.concatenate([rows[:, :half].T, rows[:, half:].T], axis=1)


def as_rows(columns, half):
    count = columns.shape[1] // 2
    pad = ((0, 0), (0, half - columns.shape[0]))
    left = jnp.pad(columns[:, :count].T, pad)
    right = jnp.pad(columns[:, count:].T, pad)
    return jnp.concatenate([left, right], axis=1)


def slot_of(tiles, devices, block_rows):
    count = tiles.shape[0]
    blocks = count // block_rows
    one_hot = (tiles[:, None] == jnp.arange(devices, dtype=jnp.int32)[None, :]).astype(jnp.bfloat16)
    one_hot = one_hot.reshape(blocks, block_rows, devices)
    positions = jnp.arange(block_rows, dtype=jnp.int32)
    lower_tri = (positions[:, None] > positions[None, :]).astype(jnp.bfloat16)
    within = jnp.einsum("ab,kbt->kat", lower_tri, one_hot, preferred_element_type=jnp.float32)
    totals = jnp.sum(one_hot.astype(jnp.float32), axis=1)
    offsets = jnp.cumsum(totals, axis=0) - totals
    before = within + offsets[:, None, :]
    rank = jnp.sum(before * one_hot.astype(jnp.float32), axis=2)
    return rank.reshape(count).astype(jnp.int32)


def on_device(
    control,
    background_std,
    diffusivity,
    land_sea,
    departures,
    obs_frac,
    obs_weight,
    obs_cell,
    obs_tile,
):
    values = control.shape[0]
    tile_lat = control.shape[1]
    tile_lon = control.shape[2]
    band_count = lax.axis_size("band")
    lon_count = lax.axis_size("lon")
    devices = band_count * lon_count
    sea = land_sea.astype(jnp.float32)
    stacked = jnp.stack([diffusivity, sea])
    depth = PASSES
    rimmed = with_halo(stacked, depth)
    lat_rows = (
        lax.axis_index("band") * tile_lat
        - depth
        + jnp.arange(tile_lat + 2 * depth, dtype=jnp.int32)
    )
    inside = ((lat_rows >= 0) & (lat_rows < band_count * tile_lat)).astype(jnp.float32)
    south, east = face_weights(rimmed[0], rimmed[1] * inside[:, None])
    state = smooth(control * sea[None], south, east)
    increment = state * background_std[:, None, None]
    count = obs_tile.shape[0]
    block_rows = 512
    blocks = count // block_rows
    capacity = 5 * count // (4 * devices)
    slots = devices * capacity
    tiles = obs_tile[:, 0]
    target = tiles * capacity + slot_of(tiles, devices, block_rows)
    target = jnp.clip(target, 0, slots - 1)
    payload = jnp.concatenate(
        [departures, obs_frac, obs_weight[None, :], obs_cell.astype(jnp.float32)[None, :]], axis=0
    )
    half = 64
    outgoing = scatter_rows(target, doubled_rows(payload, half), slots)
    arrived = as_columns(exchange_rows(outgoing), half)
    depart = arrived[:values]
    lat_frac = arrived[values]
    lon_frac = arrived[values + 1]
    row_weight = arrived[values + 2]
    cell = arrived[values + 3].astype(jnp.int32)
    lat_start = cell // (tile_lon - 1)
    lon_start = cell % (tile_lon - 1)
    lat_ids = jnp.arange(tile_lat, dtype=jnp.int32)[:, None]
    lon_ids = jnp.arange(tile_lon, dtype=jnp.int32)[:, None]
    lat_table = (lat_ids == lat_start[None, :]).astype(jnp.float32) * (1.0 - lat_frac)[None, :]
    lat_table = (
        lat_table + (lat_ids == lat_start[None, :] + 1).astype(jnp.float32) * lat_frac[None, :]
    )
    lon_table = (lon_ids == lon_start[None, :]).astype(jnp.float32) * (1.0 - lon_frac)[None, :]
    lon_table = (
        lon_table + (lon_ids == lon_start[None, :] + 1).astype(jnp.float32) * lon_frac[None, :]
    )
    partial_rows = jnp.einsum(
        "vij,jn->vin", increment, lon_table, precision=HIGH, preferred_element_type=jnp.float32
    )
    equiv = jnp.sum(partial_rows * lat_table[None, :, :], axis=1)
    misfit = row_weight * (equiv - depart)
    spread = misfit[:, None, :] * lat_table[None, :, :]
    adjoint = jnp.einsum(
        "vin,jn->vij", spread, lon_table, precision=HIGH, preferred_element_type=jnp.float32
    )
    adjoint = adjoint * background_std[:, None, None]
    gradient = control + sea[None] * smooth(adjoint, south, east)
    returned = gather_rows(target // 2, exchange_rows(as_rows(misfit, half)))
    odd = (target % 2 == 1)[:, None]
    obs_residual = jnp.where(odd, returned[:, half:], returned[:, :half])[:, :values].T
    return (gradient, obs_residual)


def solution(mesh):
    in_specs = (
        P(None, "band", "lon"),
        P(),
        P("band", "lon"),
        P("band", "lon"),
        P(None, ("band", "lon")),
        P(None, ("band", "lon")),
        P(("band", "lon")),
        P(("band", "lon")),
        P(("band", "lon"), None),
    )
    out_specs = (P(None, "band", "lon"), P(None, ("band", "lon")))
    return jax.shard_map(
        on_device, mesh=mesh, in_specs=in_specs, out_specs=out_specs, check_vma=False
    )
```

```python
import jax
import jax.numpy as jnp
from jax import lax
from jax.experimental import pallas as pl
from jax.experimental.pallas import tpu as pltpu
from jax.sharding import PartitionSpec as P

PASSES = 4


HIGH = lax.Precision.HIGH


def ring_halo(array, axis, dim, width):
    count, length = (lax.axis_size(axis), array.shape[dim])
    up = [(i, (i + 1) % count) for i in range(count)]
    down = [(j, i) for i, j in up]
    last = lax.slice_in_dim(array, length - width, length, axis=dim)
    initial = lax.slice_in_dim(array, 0, width, axis=dim)
    before = lax.ppermute(last, axis, up)
    after = lax.ppermute(initial, axis, down)
    return jnp.concatenate([before, array, after], axis=dim)


def with_halo(array, width):
    array = ring_halo(array, "band", array.ndim - 2, width)
    return ring_halo(array, "lon", array.ndim - 1, width)


def face_weights(kappa_pad, sea_pad):
    south = 0.5 * (kappa_pad[:-1, :] + kappa_pad[1:, :]) * sea_pad[:-1, :] * sea_pad[1:, :]
    east = 0.5 * (kappa_pad[:, :-1] + kappa_pad[:, 1:]) * sea_pad[:, :-1] * sea_pad[:, 1:]
    return (south, east)


def diffuse_once(field, south, east):
    flux_south = south * (field[:, 1:, :] - field[:, :-1, :])
    flux_east = east * (field[:, :, 1:] - field[:, :, :-1])
    zero_lat = ((0, 0), (0, 1), (0, 0))
    along_lat = jnp.pad(flux_south, zero_lat) - jnp.pad(flux_south, ((0, 0), (1, 0), (0, 0)))
    along_lon = jnp.pad(flux_east, ((0, 0), (0, 0), (0, 1))) - jnp.pad(flux_east, ((0, 0), (0, 0), (1, 0)))
    return field + along_lat + along_lon


def smooth(field, south, east):
    tile_lat, tile_lon = field.shape[1], field.shape[2]
    result = with_halo(field, PASSES)
    for step in range(PASSES):
        result = diffuse_once(result, south, east)
    return result[:, PASSES:PASSES + tile_lat, PASSES:PASSES + tile_lon]


def scatter_kernel(target_ref, rows_ref, out_ref):
    out_ref[...] = jnp.zeros(out_ref.shape, out_ref.dtype)

    def body(n, carry):
        out_ref[pl.ds(target_ref[n], 1), :] = rows_ref[pl.ds(n, 1), :]
        return carry

    lax.fori_loop(0, rows_ref.shape[0], body, 0, unroll=8)


def gather_kernel(source_ref, rows_ref, out_ref):
    def body(n, carry):
        out_ref[pl.ds(n, 1), :] = rows_ref[pl.ds(source_ref[n], 1), :]
        return carry

    lax.fori_loop(0, out_ref.shape[0], body, 0, unroll=8)


def scatter_rows(target, rows, slots):
    return pl.pallas_call(
        scatter_kernel,
        out_shape=jax.ShapeDtypeStruct((slots, rows.shape[1]), rows.dtype),
        in_specs=[pl.BlockSpec(memory_space=pltpu.SMEM), pl.BlockSpec(memory_space=pltpu.VMEM)],
        out_specs=pl.BlockSpec(memory_space=pltpu.VMEM),
    )(target, rows)


def gather_rows(source, rows):
    return pl.pallas_call(
        gather_kernel,
        out_shape=jax.ShapeDtypeStruct((source.shape[0], rows.shape[1]), rows.dtype),
        in_specs=[pl.BlockSpec(memory_space=pltpu.SMEM), pl.BlockSpec(memory_space=pltpu.VMEM)],
        out_specs=pl.BlockSpec(memory_space=pltpu.VMEM),
    )(source, rows)


def flat_chunks(rows, devices):
    slots, width = rows.shape
    chunk = slots // devices * width
    padded = -(-chunk // 1024) * 1024
    flat = jnp.pad(rows.reshape(devices, chunk), ((0, 0), (0, padded - chunk)))
    return flat.reshape(devices, padded // 128, 128)


def exchange_chunks(flat, slots, width):
    devices = flat.shape[0]
    chunk = slots // devices * width
    arrived = lax.all_to_all(flat, ("band", "lon"), 0, 0, tiled=True)
    return arrived.reshape(devices, -1)[:, :chunk].reshape(slots, width)


def slot_of(tiles, devices, block_rows):
    count = tiles.shape[0]
    blocks = count // block_rows
    one_hot = (tiles[:, None] == jnp.arange(devices, dtype=jnp.int32)[None, :]).astype(jnp.bfloat16)
    one_hot = one_hot.reshape(blocks, block_rows, devices)
    positions = jnp.arange(block_rows, dtype=jnp.int32)
    lower_tri = (positions[:, None] > positions[None, :]).astype(jnp.bfloat16)
    within = jnp.einsum("ab,kbt->kat", lower_tri, one_hot, preferred_element_type=jnp.float32)
    totals = jnp.sum(one_hot.astype(jnp.float32), axis=1)
    offsets = jnp.cumsum(totals, axis=0) - totals
    before = within + offsets[:, None, :]
    rank = jnp.sum(before * one_hot.astype(jnp.float32), axis=2)
    return rank.reshape(count).astype(jnp.int32)


def on_device(
    control,
    background_std,
    diffusivity,
    land_sea,
    departures,
    obs_frac,
    obs_weight,
    obs_cell,
    obs_tile,
):
    values = control.shape[0]
    tile_lat = control.shape[1]
    tile_lon = control.shape[2]
    band_count = lax.axis_size("band")
    lon_count = lax.axis_size("lon")
    devices = band_count * lon_count
    count = obs_tile.shape[0]
    block_rows = 512
    blocks = count // block_rows
    capacity = 5 * count // (4 * devices)
    slots = devices * capacity
    tiles = obs_tile[:, 0]
    target = tiles * capacity + slot_of(tiles, devices, block_rows)
    target = jnp.clip(target, 0, slots - 1)
    payload = jnp.concatenate(
        [departures, obs_frac, obs_weight[None, :], obs_cell.astype(jnp.float32)[None, :]], axis=0
    )
    outgoing = flat_chunks(scatter_rows(target, payload.T, slots), devices)
    outgoing, control, diffusivity, land_sea = lax.optimization_barrier(
        (outgoing, control, diffusivity, land_sea)
    )
    sea = land_sea.astype(jnp.float32)
    stacked = jnp.stack([diffusivity, sea])
    depth = PASSES
    rimmed = with_halo(stacked, depth)
    lat_rows = (
        lax.axis_index("band") * tile_lat
        - depth
        + jnp.arange(tile_lat + 2 * depth, dtype=jnp.int32)
    )
    inside = ((lat_rows >= 0) & (lat_rows < band_count * tile_lat)).astype(jnp.float32)
    south, east = face_weights(rimmed[0], rimmed[1] * inside[:, None])
    state = smooth(control * sea[None], south, east)
    increment = state * background_std[:, None, None]
    arrived = exchange_chunks(outgoing, slots, values + 4).T
    depart = arrived[:values]
    lat_frac = arrived[values]
    lon_frac = arrived[values + 1]
    row_weight = arrived[values + 2]
    cell = arrived[values + 3].astype(jnp.int32)
    lat_start = cell // (tile_lon - 1)
    lon_start = cell % (tile_lon - 1)
    lat_ids = jnp.arange(tile_lat, dtype=jnp.int32)[:, None]
    lon_ids = jnp.arange(tile_lon, dtype=jnp.int32)[:, None]
    lat_table = (lat_ids == lat_start[None, :]).astype(jnp.float32) * (1.0 - lat_frac)[None, :]
    lat_table = (
        lat_table + (lat_ids == lat_start[None, :] + 1).astype(jnp.float32) * lat_frac[None, :]
    )
    lon_table = (lon_ids == lon_start[None, :]).astype(jnp.float32) * (1.0 - lon_frac)[None, :]
    lon_table = (
        lon_table + (lon_ids == lon_start[None, :] + 1).astype(jnp.float32) * lon_frac[None, :]
    )
    partial_rows = jnp.einsum(
        "vij,jn->vin", increment, lon_table, precision=HIGH, preferred_element_type=jnp.float32
    )
    equiv = jnp.sum(partial_rows * lat_table[None, :, :], axis=1)
    misfit = row_weight * (equiv - depart)
    back = flat_chunks(misfit.T, devices)
    back, misfit = lax.optimization_barrier((back, misfit))
    spread = misfit[:, None, :] * lat_table[None, :, :]
    adjoint = jnp.einsum(
        "vin,jn->vij", spread, lon_table, precision=HIGH, preferred_element_type=jnp.float32
    )
    adjoint = adjoint * background_std[:, None, None]
    gradient = control + sea[None] * smooth(adjoint, south, east)
    returned = exchange_chunks(back, slots, values)
    obs_residual = gather_rows(target, returned).T
    return (gradient, obs_residual)


def solution(mesh):
    in_specs = (
        P(None, "band", "lon"),
        P(),
        P("band", "lon"),
        P("band", "lon"),
        P(None, ("band", "lon")),
        P(None, ("band", "lon")),
        P(("band", "lon")),
        P(("band", "lon")),
        P(("band", "lon"), None),
    )
    out_specs = (P(None, "band", "lon"), P(None, ("band", "lon")))
    return jax.shard_map(
        on_device, mesh=mesh, in_specs=in_specs, out_specs=out_specs, check_vma=False
    )
```

```python
import jax
import jax.numpy as jnp
from jax import lax
from jax.experimental import pallas as pl
from jax.experimental.pallas import tpu as pltpu
from jax.sharding import PartitionSpec as P

PASSES = 4


HIGH = lax.Precision.HIGH


def ring_halo(array, axis, dim, width):
    count, length = (lax.axis_size(axis), array.shape[dim])
    up = [(i, (i + 1) % count) for i in range(count)]
    down = [(j, i) for i, j in up]
    last = lax.slice_in_dim(array, length - width, length, axis=dim)
    initial = lax.slice_in_dim(array, 0, width, axis=dim)
    before = lax.ppermute(last, axis, up)
    after = lax.ppermute(initial, axis, down)
    return jnp.concatenate([before, array, after], axis=dim)


def with_halo(array, width):
    array = ring_halo(array, "band", array.ndim - 2, width)
    return ring_halo(array, "lon", array.ndim - 1, width)


def face_weights(kappa_pad, sea_pad):
    south = 0.5 * (kappa_pad[:-1, :] + kappa_pad[1:, :]) * sea_pad[:-1, :] * sea_pad[1:, :]
    east = 0.5 * (kappa_pad[:, :-1] + kappa_pad[:, 1:]) * sea_pad[:, :-1] * sea_pad[:, 1:]
    return (south, east)


def diffuse_once(field, south, east):
    flux_south = south * (field[:, 1:, :] - field[:, :-1, :])
    flux_east = east * (field[:, :, 1:] - field[:, :, :-1])
    zero_lat = ((0, 0), (0, 1), (0, 0))
    along_lat = jnp.pad(flux_south, zero_lat) - jnp.pad(flux_south, ((0, 0), (1, 0), (0, 0)))
    along_lon = jnp.pad(flux_east, ((0, 0), (0, 0), (0, 1))) - jnp.pad(flux_east, ((0, 0), (0, 0), (1, 0)))
    return field + along_lat + along_lon


def smooth(field, south, east):
    tile_lat, tile_lon = field.shape[1], field.shape[2]
    result = with_halo(field, PASSES)
    for step in range(PASSES):
        result = diffuse_once(result, south, east)
    return result[:, PASSES:PASSES + tile_lat, PASSES:PASSES + tile_lon]


def scatter_kernel(target_ref, rows_ref, out_ref):
    out_ref[...] = jnp.zeros(out_ref.shape, out_ref.dtype)

    def body(group, carry):
        first = pl.multiple_of(group * 8, 8)
        block = rows_ref[pl.ds(first, 8), :]
        for k in range(8):
            out_ref[pl.ds(target_ref[first + k], 1), :] = block[k:k + 1, :]
        return carry

    lax.fori_loop(0, rows_ref.shape[0] // 8, body, 0, unroll=2)


def gather_kernel(source_ref, rows_ref, out_ref):
    def body(group, carry):
        first = pl.multiple_of(group * 8, 8)
        parts = [rows_ref[pl.ds(source_ref[first + k], 1), :] for k in range(8)]
        out_ref[pl.ds(first, 8), :] = jnp.concatenate(parts, axis=0)
        return carry

    lax.fori_loop(0, out_ref.shape[0] // 8, body, 0, unroll=2)


def scatter_rows(target, rows, slots):
    return pl.pallas_call(
        scatter_kernel,
        out_shape=jax.ShapeDtypeStruct((slots, rows.shape[1]), rows.dtype),
        in_specs=[pl.BlockSpec(memory_space=pltpu.SMEM), pl.BlockSpec(memory_space=pltpu.VMEM)],
        out_specs=pl.BlockSpec(memory_space=pltpu.VMEM),
    )(target, rows)


def gather_rows(source, rows):
    return pl.pallas_call(
        gather_kernel,
        out_shape=jax.ShapeDtypeStruct((source.shape[0], rows.shape[1]), rows.dtype),
        in_specs=[pl.BlockSpec(memory_space=pltpu.SMEM), pl.BlockSpec(memory_space=pltpu.VMEM)],
        out_specs=pl.BlockSpec(memory_space=pltpu.VMEM),
    )(source, rows)


def flat_chunks(rows, devices):
    slots, width = rows.shape
    chunk = slots // devices * width
    padded = -(-chunk // 1024) * 1024
    flat = jnp.pad(rows.reshape(devices, chunk), ((0, 0), (0, padded - chunk)))
    return flat.reshape(devices, padded // 128, 128)


def exchange_chunks(flat, slots, width):
    devices = flat.shape[0]
    chunk = slots // devices * width
    arrived = lax.all_to_all(flat, ("band", "lon"), 0, 0, tiled=True)
    return arrived.reshape(devices, -1)[:, :chunk].reshape(slots, width)


def slot_of(tiles, devices, block_rows):
    count = tiles.shape[0]
    blocks = count // block_rows
    one_hot = (tiles[:, None] == jnp.arange(devices, dtype=jnp.int32)[None, :]).astype(jnp.bfloat16)
    one_hot = one_hot.reshape(blocks, block_rows, devices)
    positions = jnp.arange(block_rows, dtype=jnp.int32)
    lower_tri = (positions[:, None] > positions[None, :]).astype(jnp.bfloat16)
    within = jnp.einsum("ab,kbt->kat", lower_tri, one_hot, preferred_element_type=jnp.float32)
    totals = jnp.sum(one_hot.astype(jnp.float32), axis=1)
    offsets = jnp.cumsum(totals, axis=0) - totals
    before = within + offsets[:, None, :]
    rank = jnp.sum(before * one_hot.astype(jnp.float32), axis=2)
    return rank.reshape(count).astype(jnp.int32)


def on_device(
    control,
    background_std,
    diffusivity,
    land_sea,
    departures,
    obs_frac,
    obs_weight,
    obs_cell,
    obs_tile,
):
    values = control.shape[0]
    tile_lat = control.shape[1]
    tile_lon = control.shape[2]
    band_count = lax.axis_size("band")
    lon_count = lax.axis_size("lon")
    devices = band_count * lon_count
    count = obs_tile.shape[0]
    block_rows = 512
    blocks = count // block_rows
    capacity = 5 * count // (4 * devices)
    slots = devices * capacity
    tiles = obs_tile[:, 0]
    target = tiles * capacity + slot_of(tiles, devices, block_rows)
    target = jnp.clip(target, 0, slots - 1)
    payload = jnp.concatenate(
        [departures, obs_frac, obs_weight[None, :], obs_cell.astype(jnp.float32)[None, :]], axis=0
    )
    outgoing = flat_chunks(scatter_rows(target, payload.T, slots), devices)
    outgoing, control, diffusivity, land_sea = lax.optimization_barrier(
        (outgoing, control, diffusivity, land_sea)
    )
    sea = land_sea.astype(jnp.float32)
    stacked = jnp.stack([diffusivity, sea])
    depth = PASSES
    rimmed = with_halo(stacked, depth)
    lat_rows = (
        lax.axis_index("band") * tile_lat
        - depth
        + jnp.arange(tile_lat + 2 * depth, dtype=jnp.int32)
    )
    inside = ((lat_rows >= 0) & (lat_rows < band_count * tile_lat)).astype(jnp.float32)
    south, east = face_weights(rimmed[0], rimmed[1] * inside[:, None])
    state = smooth(control * sea[None], south, east)
    increment = state * background_std[:, None, None]
    arrived = exchange_chunks(outgoing, slots, values + 4).T
    depart = arrived[:values]
    lat_frac = arrived[values]
    lon_frac = arrived[values + 1]
    row_weight = arrived[values + 2]
    cell = arrived[values + 3].astype(jnp.int32)
    lat_start = cell // (tile_lon - 1)
    lon_start = cell % (tile_lon - 1)
    lat_ids = jnp.arange(tile_lat, dtype=jnp.int32)[:, None]
    lon_ids = jnp.arange(tile_lon, dtype=jnp.int32)[:, None]
    lat_table = (lat_ids == lat_start[None, :]).astype(jnp.float32) * (1.0 - lat_frac)[None, :]
    lat_table = (
        lat_table + (lat_ids == lat_start[None, :] + 1).astype(jnp.float32) * lat_frac[None, :]
    )
    lon_table = (lon_ids == lon_start[None, :]).astype(jnp.float32) * (1.0 - lon_frac)[None, :]
    lon_table = (
        lon_table + (lon_ids == lon_start[None, :] + 1).astype(jnp.float32) * lon_frac[None, :]
    )
    partial_rows = jnp.einsum(
        "vij,jn->vin", increment, lon_table, precision=HIGH, preferred_element_type=jnp.float32
    )
    equiv = jnp.sum(partial_rows * lat_table[None, :, :], axis=1)
    misfit = row_weight * (equiv - depart)
    back = flat_chunks(misfit.T, devices)
    back, misfit = lax.optimization_barrier((back, misfit))
    spread = misfit[:, None, :] * lat_table[None, :, :]
    adjoint = jnp.einsum(
        "vin,jn->vij", spread, lon_table, precision=HIGH, preferred_element_type=jnp.float32
    )
    adjoint = adjoint * background_std[:, None, None]
    gradient = control + sea[None] * smooth(adjoint, south, east)
    returned = exchange_chunks(back, slots, values)
    obs_residual = gather_rows(target, returned).T
    return (gradient, obs_residual)


def solution(mesh):
    in_specs = (
        P(None, "band", "lon"),
        P(),
        P("band", "lon"),
        P("band", "lon"),
        P(None, ("band", "lon")),
        P(None, ("band", "lon")),
        P(("band", "lon")),
        P(("band", "lon")),
        P(("band", "lon"), None),
    )
    out_specs = (P(None, "band", "lon"), P(None, ("band", "lon")))
    return jax.shard_map(
        on_device, mesh=mesh, in_specs=in_specs, out_specs=out_specs, check_vma=False
    )
```

```python
import jax
import jax.numpy as jnp
from jax import lax
from jax.experimental import pallas as pl
from jax.experimental.pallas import tpu as pltpu
from jax.sharding import PartitionSpec as P

PASSES = 4


HIGH = lax.Precision.HIGH


def ring_halo(array, axis, dim, width):
    count, length = (lax.axis_size(axis), array.shape[dim])
    up = [(i, (i + 1) % count) for i in range(count)]
    down = [(j, i) for i, j in up]
    last = lax.slice_in_dim(array, length - width, length, axis=dim)
    initial = lax.slice_in_dim(array, 0, width, axis=dim)
    before = lax.ppermute(last, axis, up)
    after = lax.ppermute(initial, axis, down)
    return jnp.concatenate([before, array, after], axis=dim)


def with_halo(array, width):
    array = ring_halo(array, "band", array.ndim - 2, width)
    return ring_halo(array, "lon", array.ndim - 1, width)


def face_weights(kappa_pad, sea_pad):
    south = 0.5 * (kappa_pad[:-1, :] + kappa_pad[1:, :]) * sea_pad[:-1, :] * sea_pad[1:, :]
    east = 0.5 * (kappa_pad[:, :-1] + kappa_pad[:, 1:]) * sea_pad[:, :-1] * sea_pad[:, 1:]
    return (south, east)


def diffuse_once(field, south, east):
    flux_south = south * (field[:, 1:, :] - field[:, :-1, :])
    flux_east = east * (field[:, :, 1:] - field[:, :, :-1])
    zero_lat = ((0, 0), (0, 1), (0, 0))
    along_lat = jnp.pad(flux_south, zero_lat) - jnp.pad(flux_south, ((0, 0), (1, 0), (0, 0)))
    along_lon = jnp.pad(flux_east, ((0, 0), (0, 0), (0, 1))) - jnp.pad(flux_east, ((0, 0), (0, 0), (1, 0)))
    return field + along_lat + along_lon


def smooth_padded(result, south, east):
    tile_lat, tile_lon = result.shape[1] - 2 * PASSES, result.shape[2] - 2 * PASSES
    for step in range(PASSES):
        result = diffuse_once(result, south, east)
    return result[:, PASSES:PASSES + tile_lat, PASSES:PASSES + tile_lon]


def smooth(field, south, east):
    return smooth_padded(with_halo(field, PASSES), south, east)


def scatter_kernel(target_ref, rows_ref, out_ref):
    out_ref[...] = jnp.zeros(out_ref.shape, out_ref.dtype)

    def body(group, carry):
        first = pl.multiple_of(group * 8, 8)
        block = rows_ref[pl.ds(first, 8), :]
        for k in range(8):
            out_ref[pl.ds(target_ref[first + k], 1), :] = block[k:k + 1, :]
        return carry

    lax.fori_loop(0, rows_ref.shape[0] // 8, body, 0, unroll=2)


def gather_kernel(source_ref, rows_ref, out_ref):
    def body(group, carry):
        first = pl.multiple_of(group * 8, 8)
        parts = [rows_ref[pl.ds(source_ref[first + k], 1), :] for k in range(8)]
        out_ref[pl.ds(first, 8), :] = jnp.concatenate(parts, axis=0)
        return carry

    lax.fori_loop(0, out_ref.shape[0] // 8, body, 0, unroll=2)


def scatter_rows(target, rows, slots):
    return pl.pallas_call(
        scatter_kernel,
        out_shape=jax.ShapeDtypeStruct((slots, rows.shape[1]), rows.dtype),
        in_specs=[pl.BlockSpec(memory_space=pltpu.SMEM), pl.BlockSpec(memory_space=pltpu.VMEM)],
        out_specs=pl.BlockSpec(memory_space=pltpu.VMEM),
    )(target, rows)


def gather_rows(source, rows):
    return pl.pallas_call(
        gather_kernel,
        out_shape=jax.ShapeDtypeStruct((source.shape[0], rows.shape[1]), rows.dtype),
        in_specs=[pl.BlockSpec(memory_space=pltpu.SMEM), pl.BlockSpec(memory_space=pltpu.VMEM)],
        out_specs=pl.BlockSpec(memory_space=pltpu.VMEM),
    )(source, rows)


def flat_chunks(rows, devices):
    slots, width = rows.shape
    chunk = slots // devices * width
    padded = -(-chunk // 1024) * 1024
    flat = jnp.pad(rows.reshape(devices, chunk), ((0, 0), (0, padded - chunk)))
    return flat.reshape(devices, padded // 128, 128)


def exchange_chunks(flat, slots, width):
    devices = flat.shape[0]
    chunk = slots // devices * width
    arrived = lax.all_to_all(flat, ("band", "lon"), 0, 0, tiled=True)
    return arrived.reshape(devices, -1)[:, :chunk].reshape(slots, width)


def slot_of(tiles, devices, block_rows):
    count = tiles.shape[0]
    blocks = count // block_rows
    one_hot = (tiles[:, None] == jnp.arange(devices, dtype=jnp.int32)[None, :]).astype(jnp.bfloat16)
    one_hot = one_hot.reshape(blocks, block_rows, devices)
    positions = jnp.arange(block_rows, dtype=jnp.int32)
    lower_tri = (positions[:, None] > positions[None, :]).astype(jnp.bfloat16)
    within = jnp.einsum("ab,kbt->kat", lower_tri, one_hot, preferred_element_type=jnp.float32)
    totals = jnp.sum(one_hot.astype(jnp.float32), axis=1)
    offsets = jnp.cumsum(totals, axis=0) - totals
    before = within + offsets[:, None, :]
    rank = jnp.sum(before * one_hot.astype(jnp.float32), axis=2)
    return rank.reshape(count).astype(jnp.int32)


def on_device(
    control,
    background_std,
    diffusivity,
    land_sea,
    departures,
    obs_frac,
    obs_weight,
    obs_cell,
    obs_tile,
):
    values = control.shape[0]
    tile_lat = control.shape[1]
    tile_lon = control.shape[2]
    band_count = lax.axis_size("band")
    lon_count = lax.axis_size("lon")
    devices = band_count * lon_count
    count = obs_tile.shape[0]
    block_rows = 512
    blocks = count // block_rows
    capacity = 5 * count // (4 * devices)
    slots = devices * capacity
    tiles = obs_tile[:, 0]
    target = tiles * capacity + slot_of(tiles, devices, block_rows)
    target = jnp.clip(target, 0, slots - 1)
    payload = jnp.concatenate(
        [departures, obs_frac, obs_weight[None, :], obs_cell.astype(jnp.float32)[None, :]], axis=0
    )
    outgoing = flat_chunks(scatter_rows(target, payload.T, slots), devices)
    outgoing, control, diffusivity, land_sea = lax.optimization_barrier(
        (outgoing, control, diffusivity, land_sea)
    )
    sea = land_sea.astype(jnp.float32)
    depth = PASSES
    stacked = jnp.concatenate([control * sea[None], diffusivity[None], sea[None]], axis=0)
    rimmed = with_halo(stacked, depth)
    lat_rows = (
        lax.axis_index("band") * tile_lat
        - depth
        + jnp.arange(tile_lat + 2 * depth, dtype=jnp.int32)
    )
    inside = ((lat_rows >= 0) & (lat_rows < band_count * tile_lat)).astype(jnp.float32)
    south, east = face_weights(rimmed[values], rimmed[values + 1] * inside[:, None])
    state = smooth_padded(rimmed[:values], south, east)
    increment = state * background_std[:, None, None]
    arrived = exchange_chunks(outgoing, slots, values + 4).T
    depart = arrived[:values]
    lat_frac = arrived[values]
    lon_frac = arrived[values + 1]
    row_weight = arrived[values + 2]
    cell = arrived[values + 3].astype(jnp.int32)
    lat_start = cell // (tile_lon - 1)
    lon_start = cell % (tile_lon - 1)
    lat_ids = jnp.arange(tile_lat, dtype=jnp.int32)[:, None]
    lon_ids = jnp.arange(tile_lon, dtype=jnp.int32)[:, None]
    lat_table = (lat_ids == lat_start[None, :]).astype(jnp.float32) * (1.0 - lat_frac)[None, :]
    lat_table = (
        lat_table + (lat_ids == lat_start[None, :] + 1).astype(jnp.float32) * lat_frac[None, :]
    )
    lon_table = (lon_ids == lon_start[None, :]).astype(jnp.float32) * (1.0 - lon_frac)[None, :]
    lon_table = (
        lon_table + (lon_ids == lon_start[None, :] + 1).astype(jnp.float32) * lon_frac[None, :]
    )
    partial_rows = jnp.einsum(
        "vij,jn->vin", increment, lon_table, precision=HIGH, preferred_element_type=jnp.float32
    )
    equiv = jnp.sum(partial_rows * lat_table[None, :, :], axis=1)
    misfit = row_weight * (equiv - depart)
    back = flat_chunks(misfit.T, devices)
    back, misfit = lax.optimization_barrier((back, misfit))
    spread = misfit[:, None, :] * lat_table[None, :, :]
    adjoint = jnp.einsum(
        "vin,jn->vij", spread, lon_table, precision=HIGH, preferred_element_type=jnp.float32
    )
    adjoint = adjoint * background_std[:, None, None]
    gradient = control + sea[None] * smooth(adjoint, south, east)
    returned = exchange_chunks(back, slots, values)
    obs_residual = gather_rows(target, returned).T
    return (gradient, obs_residual)


def solution(mesh):
    in_specs = (
        P(None, "band", "lon"),
        P(),
        P("band", "lon"),
        P("band", "lon"),
        P(None, ("band", "lon")),
        P(None, ("band", "lon")),
        P(("band", "lon")),
        P(("band", "lon")),
        P(("band", "lon"), None),
    )
    out_specs = (P(None, "band", "lon"), P(None, ("band", "lon")))
    return jax.shard_map(
        on_device, mesh=mesh, in_specs=in_specs, out_specs=out_specs, check_vma=False
    )
```

```python
import jax
import jax.numpy as jnp
from jax import lax
from jax.experimental import pallas as pl
from jax.experimental.pallas import tpu as pltpu
from jax.sharding import PartitionSpec as P

PASSES = 4


HIGH = lax.Precision.HIGH


def ring_halo(array, axis, dim, width):
    count, length = (lax.axis_size(axis), array.shape[dim])
    up = [(i, (i + 1) % count) for i in range(count)]
    down = [(j, i) for i, j in up]
    last = lax.slice_in_dim(array, length - width, length, axis=dim)
    initial = lax.slice_in_dim(array, 0, width, axis=dim)
    before = lax.ppermute(last, axis, up)
    after = lax.ppermute(initial, axis, down)
    return jnp.concatenate([before, array, after], axis=dim)


def with_halo(array, width):
    array = ring_halo(array, "band", array.ndim - 2, width)
    return ring_halo(array, "lon", array.ndim - 1, width)


def face_weights(kappa_pad, sea_pad):
    south = 0.5 * (kappa_pad[:-1, :] + kappa_pad[1:, :]) * sea_pad[:-1, :] * sea_pad[1:, :]
    east = 0.5 * (kappa_pad[:, :-1] + kappa_pad[:, 1:]) * sea_pad[:, :-1] * sea_pad[:, 1:]
    return (south, east)


def diffuse_once(field, south, east):
    flux_south = south * (field[:, 1:, :] - field[:, :-1, :])
    flux_east = east * (field[:, :, 1:] - field[:, :, :-1])
    zero_lat = ((0, 0), (0, 1), (0, 0))
    along_lat = jnp.pad(flux_south, zero_lat) - jnp.pad(flux_south, ((0, 0), (1, 0), (0, 0)))
    along_lon = jnp.pad(flux_east, ((0, 0), (0, 0), (0, 1))) - jnp.pad(flux_east, ((0, 0), (0, 0), (1, 0)))
    return field + along_lat + along_lon


def smooth_padded(result, south, east):
    tile_lat, tile_lon = result.shape[1] - 2 * PASSES, result.shape[2] - 2 * PASSES
    for step in range(PASSES):
        result = diffuse_once(result, south, east)
    return result[:, PASSES:PASSES + tile_lat, PASSES:PASSES + tile_lon]


def smooth(field, south, east):
    return smooth_padded(with_halo(field, PASSES), south, east)


def scatter_kernel(target_ref, rows_ref, out_ref):
    out_ref[...] = jnp.zeros(out_ref.shape, out_ref.dtype)

    def body(group, carry):
        first = pl.multiple_of(group * 8, 8)
        block = rows_ref[pl.ds(first, 8), :]
        for k in range(8):
            out_ref[pl.ds(target_ref[first + k], 1), :] = block[k:k + 1, :]
        return carry

    lax.fori_loop(0, rows_ref.shape[0] // 8, body, 0, unroll=2)


def gather_kernel(source_ref, rows_ref, out_ref):
    def body(group, carry):
        first = pl.multiple_of(group * 8, 8)
        parts = [rows_ref[pl.ds(source_ref[first + k], 1), :] for k in range(8)]
        out_ref[pl.ds(first, 8), :] = jnp.concatenate(parts, axis=0)
        return carry

    lax.fori_loop(0, out_ref.shape[0] // 8, body, 0, unroll=2)


def gather_flat_kernel(row_ref, shift_ref, flat_ref, out_ref):
    lanes = lax.broadcasted_iota(jnp.int32, (1, flat_ref.shape[1]), 1)
    width = flat_ref.shape[1]

    def body(group, carry):
        first = pl.multiple_of(group * 8, 8)
        parts = []
        for k in range(8):
            row = row_ref[first + k]
            turn = (width - shift_ref[first + k]) % width
            head = pltpu.roll(flat_ref[pl.ds(row, 1), :], turn, 1)
            tail = pltpu.roll(flat_ref[pl.ds(row + 1, 1), :], turn, 1)
            parts.append(jnp.where(lanes < jnp.where(turn == 0, width, turn), head, tail))
        out_ref[pl.ds(first, 8), :] = jnp.concatenate(parts, axis=0)
        return carry

    lax.fori_loop(0, out_ref.shape[0] // 8, body, 0, unroll=2)


def gather_flat(target, flat, capacity, width):
    chunk_rows = flat.shape[1]
    rows = flat.reshape(-1, flat.shape[2])
    offset = (target % capacity) * width
    row = (target // capacity) * chunk_rows + offset // 128
    smem = pl.BlockSpec(memory_space=pltpu.SMEM)
    return pl.pallas_call(
        gather_flat_kernel,
        out_shape=jax.ShapeDtypeStruct((target.shape[0], rows.shape[1]), rows.dtype),
        in_specs=[smem, smem, pl.BlockSpec(memory_space=pltpu.VMEM)],
        out_specs=pl.BlockSpec(memory_space=pltpu.VMEM),
    )(row, offset % 128, rows)


def scatter_rows(target, rows, slots):
    return pl.pallas_call(
        scatter_kernel,
        out_shape=jax.ShapeDtypeStruct((slots, rows.shape[1]), rows.dtype),
        in_specs=[pl.BlockSpec(memory_space=pltpu.SMEM), pl.BlockSpec(memory_space=pltpu.VMEM)],
        out_specs=pl.BlockSpec(memory_space=pltpu.VMEM),
    )(target, rows)


def gather_rows(source, rows):
    return pl.pallas_call(
        gather_kernel,
        out_shape=jax.ShapeDtypeStruct((source.shape[0], rows.shape[1]), rows.dtype),
        in_specs=[pl.BlockSpec(memory_space=pltpu.SMEM), pl.BlockSpec(memory_space=pltpu.VMEM)],
        out_specs=pl.BlockSpec(memory_space=pltpu.VMEM),
    )(source, rows)


def flat_chunks(rows, devices):
    slots, width = rows.shape
    chunk = slots // devices * width
    padded = -(-chunk // 1024) * 1024
    flat = jnp.pad(rows.reshape(devices, chunk), ((0, 0), (0, padded - chunk)))
    return flat.reshape(devices, padded // 128, 128)


def exchange_chunks(flat, slots, width):
    devices = flat.shape[0]
    chunk = slots // devices * width
    arrived = lax.all_to_all(flat, ("band", "lon"), 0, 0, tiled=True)
    return arrived.reshape(devices, -1)[:, :chunk].reshape(slots, width)


def slot_of(tiles, devices, block_rows):
    count = tiles.shape[0]
    blocks = count // block_rows
    one_hot = (tiles[:, None] == jnp.arange(devices, dtype=jnp.int32)[None, :]).astype(jnp.bfloat16)
    one_hot = one_hot.reshape(blocks, block_rows, devices)
    positions = jnp.arange(block_rows, dtype=jnp.int32)
    lower_tri = (positions[:, None] > positions[None, :]).astype(jnp.bfloat16)
    within = jnp.einsum("ab,kbt->kat", lower_tri, one_hot, preferred_element_type=jnp.float32)
    totals = jnp.sum(one_hot.astype(jnp.float32), axis=1)
    offsets = jnp.cumsum(totals, axis=0) - totals
    before = within + offsets[:, None, :]
    rank = jnp.sum(before * one_hot.astype(jnp.float32), axis=2)
    return rank.reshape(count).astype(jnp.int32)


def on_device(
    control,
    background_std,
    diffusivity,
    land_sea,
    departures,
    obs_frac,
    obs_weight,
    obs_cell,
    obs_tile,
):
    values = control.shape[0]
    tile_lat = control.shape[1]
    tile_lon = control.shape[2]
    band_count = lax.axis_size("band")
    lon_count = lax.axis_size("lon")
    devices = band_count * lon_count
    count = obs_tile.shape[0]
    block_rows = 512
    blocks = count // block_rows
    capacity = 5 * count // (4 * devices)
    slots = devices * capacity
    tiles = obs_tile[:, 0]
    target = tiles * capacity + slot_of(tiles, devices, block_rows)
    target = jnp.clip(target, 0, slots - 1)
    payload = jnp.concatenate(
        [departures, obs_frac, obs_weight[None, :], obs_cell.astype(jnp.float32)[None, :]], axis=0
    )
    outgoing = flat_chunks(scatter_rows(target, payload.T, slots), devices)
    outgoing, control, diffusivity, land_sea = lax.optimization_barrier(
        (outgoing, control, diffusivity, land_sea)
    )
    sea = land_sea.astype(jnp.float32)
    depth = PASSES
    stacked = jnp.concatenate([control * sea[None], diffusivity[None], sea[None]], axis=0)
    rimmed = with_halo(stacked, depth)
    lat_rows = (
        lax.axis_index("band") * tile_lat
        - depth
        + jnp.arange(tile_lat + 2 * depth, dtype=jnp.int32)
    )
    inside = ((lat_rows >= 0) & (lat_rows < band_count * tile_lat)).astype(jnp.float32)
    south, east = face_weights(rimmed[values], rimmed[values + 1] * inside[:, None])
    state = smooth_padded(rimmed[:values], south, east)
    increment = state * background_std[:, None, None]
    arrived = exchange_chunks(outgoing, slots, values + 4).T
    depart = arrived[:values]
    lat_frac = arrived[values]
    lon_frac = arrived[values + 1]
    row_weight = arrived[values + 2]
    cell = arrived[values + 3].astype(jnp.int32)
    lat_start = cell // (tile_lon - 1)
    lon_start = cell % (tile_lon - 1)
    lat_ids = jnp.arange(tile_lat, dtype=jnp.int32)[:, None]
    lon_ids = jnp.arange(tile_lon, dtype=jnp.int32)[:, None]
    lat_table = (lat_ids == lat_start[None, :]).astype(jnp.float32) * (1.0 - lat_frac)[None, :]
    lat_table = (
        lat_table + (lat_ids == lat_start[None, :] + 1).astype(jnp.float32) * lat_frac[None, :]
    )
    lon_table = (lon_ids == lon_start[None, :]).astype(jnp.float32) * (1.0 - lon_frac)[None, :]
    lon_table = (
        lon_table + (lon_ids == lon_start[None, :] + 1).astype(jnp.float32) * lon_frac[None, :]
    )
    partial_rows = jnp.einsum(
        "vij,jn->vin", increment, lon_table, precision=HIGH, preferred_element_type=jnp.float32
    )
    equiv = jnp.sum(partial_rows * lat_table[None, :, :], axis=1)
    misfit = row_weight * (equiv - depart)
    back = flat_chunks(misfit.T, devices)
    back, misfit = lax.optimization_barrier((back, misfit))
    spread = misfit[:, None, :] * lat_table[None, :, :]
    adjoint = jnp.einsum(
        "vin,jn->vij", spread, lon_table, precision=HIGH, preferred_element_type=jnp.float32
    )
    adjoint = adjoint * background_std[:, None, None]
    gradient = control + sea[None] * smooth(adjoint, south, east)
    returned = lax.all_to_all(back, ("band", "lon"), 0, 0, tiled=True)
    obs_residual = gather_flat(target, returned, capacity, values)[:, :values].T
    return (gradient, obs_residual)


def solution(mesh):
    in_specs = (
        P(None, "band", "lon"),
        P(),
        P("band", "lon"),
        P("band", "lon"),
        P(None, ("band", "lon")),
        P(None, ("band", "lon")),
        P(("band", "lon")),
        P(("band", "lon")),
        P(("band", "lon"), None),
    )
    out_specs = (P(None, "band", "lon"), P(None, ("band", "lon")))
    return jax.shard_map(
        on_device, mesh=mesh, in_specs=in_specs, out_specs=out_specs, check_vma=False
    )
```

```python
import jax
import jax.numpy as jnp
from jax import lax
from jax.experimental import pallas as pl
from jax.experimental.pallas import tpu as pltpu
from jax.sharding import PartitionSpec as P

PASSES = 4


HIGH = lax.Precision.HIGH


def ring_halo(array, axis, dim, width):
    count, length = (lax.axis_size(axis), array.shape[dim])
    up = [(i, (i + 1) % count) for i in range(count)]
    down = [(j, i) for i, j in up]
    last = lax.slice_in_dim(array, length - width, length, axis=dim)
    initial = lax.slice_in_dim(array, 0, width, axis=dim)
    before = lax.ppermute(last, axis, up)
    after = lax.ppermute(initial, axis, down)
    return jnp.concatenate([before, array, after], axis=dim)


def with_halo(array, width):
    array = ring_halo(array, "band", array.ndim - 2, width)
    return ring_halo(array, "lon", array.ndim - 1, width)


def face_weights(kappa_pad, sea_pad):
    south = 0.5 * (kappa_pad[:-1, :] + kappa_pad[1:, :]) * sea_pad[:-1, :] * sea_pad[1:, :]
    east = 0.5 * (kappa_pad[:, :-1] + kappa_pad[:, 1:]) * sea_pad[:, :-1] * sea_pad[:, 1:]
    return (south, east)


def diffuse_once(field, south, east):
    flux_south = south * (field[:, 1:, :] - field[:, :-1, :])
    flux_east = east * (field[:, :, 1:] - field[:, :, :-1])
    zero_lat = ((0, 0), (0, 1), (0, 0))
    along_lat = jnp.pad(flux_south, zero_lat) - jnp.pad(flux_south, ((0, 0), (1, 0), (0, 0)))
    along_lon = jnp.pad(flux_east, ((0, 0), (0, 0), (0, 1))) - jnp.pad(flux_east, ((0, 0), (0, 0), (1, 0)))
    return field + along_lat + along_lon


def smooth_padded(result, south, east):
    tile_lat, tile_lon = result.shape[1] - 2 * PASSES, result.shape[2] - 2 * PASSES
    result = lax.fori_loop(0, PASSES, lambda step, field: diffuse_once(field, south, east), result)
    return result[:, PASSES:PASSES + tile_lat, PASSES:PASSES + tile_lon]


def smooth(field, south, east):
    return smooth_padded(with_halo(field, PASSES), south, east)


def scatter_kernel(target_ref, rows_ref, out_ref):
    out_ref[...] = jnp.zeros(out_ref.shape, out_ref.dtype)

    def body(group, carry):
        first = pl.multiple_of(group * 8, 8)
        block = rows_ref[pl.ds(first, 8), :]
        for k in range(8):
            out_ref[pl.ds(target_ref[first + k], 1), :] = block[k:k + 1, :]
        return carry

    lax.fori_loop(0, rows_ref.shape[0] // 8, body, 0, unroll=2)


def gather_kernel(source_ref, rows_ref, out_ref):
    def body(group, carry):
        first = pl.multiple_of(group * 8, 8)
        parts = [rows_ref[pl.ds(source_ref[first + k], 1), :] for k in range(8)]
        out_ref[pl.ds(first, 8), :] = jnp.concatenate(parts, axis=0)
        return carry

    lax.fori_loop(0, out_ref.shape[0] // 8, body, 0, unroll=2)


def scatter_rows(target, rows, slots):
    return pl.pallas_call(
        scatter_kernel,
        out_shape=jax.ShapeDtypeStruct((slots, rows.shape[1]), rows.dtype),
        in_specs=[pl.BlockSpec(memory_space=pltpu.SMEM), pl.BlockSpec(memory_space=pltpu.VMEM)],
        out_specs=pl.BlockSpec(memory_space=pltpu.VMEM),
    )(target, rows)


def gather_rows(source, rows):
    return pl.pallas_call(
        gather_kernel,
        out_shape=jax.ShapeDtypeStruct((source.shape[0], rows.shape[1]), rows.dtype),
        in_specs=[pl.BlockSpec(memory_space=pltpu.SMEM), pl.BlockSpec(memory_space=pltpu.VMEM)],
        out_specs=pl.BlockSpec(memory_space=pltpu.VMEM),
    )(source, rows)


def flat_chunks(rows, devices):
    slots, width = rows.shape
    chunk = slots // devices * width
    padded = -(-chunk // 1024) * 1024
    flat = jnp.pad(rows.reshape(devices, chunk), ((0, 0), (0, padded - chunk)))
    return flat.reshape(devices, padded // 128, 128)


def exchange_chunks(flat, slots, width):
    devices = flat.shape[0]
    chunk = slots // devices * width
    arrived = lax.all_to_all(flat, ("band", "lon"), 0, 0, tiled=True)
    return arrived.reshape(devices, -1)[:, :chunk].reshape(slots, width)


def slot_of(tiles, devices, block_rows):
    count = tiles.shape[0]
    blocks = count // block_rows
    one_hot = (tiles[:, None] == jnp.arange(devices, dtype=jnp.int32)[None, :]).astype(jnp.bfloat16)
    one_hot = one_hot.reshape(blocks, block_rows, devices)
    positions = jnp.arange(block_rows, dtype=jnp.int32)
    lower_tri = (positions[:, None] > positions[None, :]).astype(jnp.bfloat16)
    within = jnp.einsum("ab,kbt->kat", lower_tri, one_hot, preferred_element_type=jnp.float32)
    totals = jnp.sum(one_hot.astype(jnp.float32), axis=1)
    offsets = jnp.cumsum(totals, axis=0) - totals
    before = within + offsets[:, None, :]
    rank = jnp.sum(before * one_hot.astype(jnp.float32), axis=2)
    return rank.reshape(count).astype(jnp.int32)


def on_device(
    control,
    background_std,
    diffusivity,
    land_sea,
    departures,
    obs_frac,
    obs_weight,
    obs_cell,
    obs_tile,
):
    values = control.shape[0]
    tile_lat = control.shape[1]
    tile_lon = control.shape[2]
    band_count = lax.axis_size("band")
    lon_count = lax.axis_size("lon")
    devices = band_count * lon_count
    count = obs_tile.shape[0]
    block_rows = 512
    blocks = count // block_rows
    capacity = 5 * count // (4 * devices)
    slots = devices * capacity
    tiles = obs_tile[:, 0]
    target = tiles * capacity + slot_of(tiles, devices, block_rows)
    target = jnp.clip(target, 0, slots - 1)
    payload = jnp.concatenate(
        [departures, obs_frac, obs_weight[None, :], obs_cell.astype(jnp.float32)[None, :]], axis=0
    )
    outgoing = flat_chunks(scatter_rows(target, payload.T, slots), devices)
    outgoing, control, diffusivity, land_sea = lax.optimization_barrier(
        (outgoing, control, diffusivity, land_sea)
    )
    sea = land_sea.astype(jnp.float32)
    depth = PASSES
    stacked = jnp.concatenate([control * sea[None], diffusivity[None], sea[None]], axis=0)
    rimmed = with_halo(stacked, depth)
    lat_rows = (
        lax.axis_index("band") * tile_lat
        - depth
        + jnp.arange(tile_lat + 2 * depth, dtype=jnp.int32)
    )
    inside = ((lat_rows >= 0) & (lat_rows < band_count * tile_lat)).astype(jnp.float32)
    south, east = face_weights(rimmed[values], rimmed[values + 1] * inside[:, None])
    state = smooth_padded(rimmed[:values], south, east)
    increment = state * background_std[:, None, None]
    arrived = exchange_chunks(outgoing, slots, values + 4).T
    depart = arrived[:values]
    lat_frac = arrived[values]
    lon_frac = arrived[values + 1]
    row_weight = arrived[values + 2]
    cell = arrived[values + 3].astype(jnp.int32)
    lat_start = cell // (tile_lon - 1)
    lon_start = cell % (tile_lon - 1)
    lat_ids = jnp.arange(tile_lat, dtype=jnp.int32)[:, None]
    lon_ids = jnp.arange(tile_lon, dtype=jnp.int32)[:, None]
    lat_table = (lat_ids == lat_start[None, :]).astype(jnp.float32) * (1.0 - lat_frac)[None, :]
    lat_table = (
        lat_table + (lat_ids == lat_start[None, :] + 1).astype(jnp.float32) * lat_frac[None, :]
    )
    lon_table = (lon_ids == lon_start[None, :]).astype(jnp.float32) * (1.0 - lon_frac)[None, :]
    lon_table = (
        lon_table + (lon_ids == lon_start[None, :] + 1).astype(jnp.float32) * lon_frac[None, :]
    )
    partial_rows = jnp.einsum(
        "vij,jn->vin", increment, lon_table, precision=HIGH, preferred_element_type=jnp.float32
    )
    equiv = jnp.sum(partial_rows * lat_table[None, :, :], axis=1)
    misfit = row_weight * (equiv - depart)
    back = flat_chunks(misfit.T, devices)
    back, misfit = lax.optimization_barrier((back, misfit))
    spread = misfit[:, None, :] * lat_table[None, :, :]
    adjoint = jnp.einsum(
        "vin,jn->vij", spread, lon_table, precision=HIGH, preferred_element_type=jnp.float32
    )
    adjoint = adjoint * background_std[:, None, None]
    gradient = control + sea[None] * smooth(adjoint, south, east)
    returned = exchange_chunks(back, slots, values)
    obs_residual = gather_rows(target, returned).T
    return (gradient, obs_residual)


def solution(mesh):
    in_specs = (
        P(None, "band", "lon"),
        P(),
        P("band", "lon"),
        P("band", "lon"),
        P(None, ("band", "lon")),
        P(None, ("band", "lon")),
        P(("band", "lon")),
        P(("band", "lon")),
        P(("band", "lon"), None),
    )
    out_specs = (P(None, "band", "lon"), P(None, ("band", "lon")))
    return jax.shard_map(
        on_device, mesh=mesh, in_specs=in_specs, out_specs=out_specs, check_vma=False
    )
```

```python
import jax
import jax.numpy as jnp
from jax import lax
from jax.experimental import pallas as pl
from jax.experimental.pallas import tpu as pltpu
from jax.sharding import PartitionSpec as P

PASSES = 4


HIGH = lax.Precision.HIGH


def ring_halo(array, axis, dim, width):
    count, length = (lax.axis_size(axis), array.shape[dim])
    up = [(i, (i + 1) % count) for i in range(count)]
    down = [(j, i) for i, j in up]
    last = lax.slice_in_dim(array, length - width, length, axis=dim)
    initial = lax.slice_in_dim(array, 0, width, axis=dim)
    before = lax.ppermute(last, axis, up)
    after = lax.ppermute(initial, axis, down)
    return jnp.concatenate([before, array, after], axis=dim)


def with_halo(array, width):
    array = ring_halo(array, "band", array.ndim - 2, width)
    return ring_halo(array, "lon", array.ndim - 1, width)


def face_weights(kappa_pad, sea_pad):
    south = 0.5 * (kappa_pad[:-1, :] + kappa_pad[1:, :]) * sea_pad[:-1, :] * sea_pad[1:, :]
    east = 0.5 * (kappa_pad[:, :-1] + kappa_pad[:, 1:]) * sea_pad[:, :-1] * sea_pad[:, 1:]
    return (south, east)


def diffuse_once(field, south, east):
    flux_south = south * (field[:, 1:, :] - field[:, :-1, :])
    flux_east = east * (field[:, :, 1:] - field[:, :, :-1])
    zero_lat = ((0, 0), (0, 1), (0, 0))
    along_lat = jnp.pad(flux_south, zero_lat) - jnp.pad(flux_south, ((0, 0), (1, 0), (0, 0)))
    along_lon = jnp.pad(flux_east, ((0, 0), (0, 0), (0, 1))) - jnp.pad(flux_east, ((0, 0), (0, 0), (1, 0)))
    return field + along_lat + along_lon


def smooth_padded(result, south, east):
    tile_lat, tile_lon = result.shape[1] - 2 * PASSES, result.shape[2] - 2 * PASSES
    result = lax.fori_loop(0, PASSES, lambda step, field: diffuse_once(field, south, east), result)
    return result[:, PASSES:PASSES + tile_lat, PASSES:PASSES + tile_lon]


def smooth(field, south, east):
    return smooth_padded(with_halo(field, PASSES), south, east)


def scatter_kernel(target_ref, rows_ref, out_ref):
    out_ref[...] = jnp.zeros(out_ref.shape, out_ref.dtype)

    def body(group, carry):
        first = pl.multiple_of(group * 8, 8)
        block = rows_ref[pl.ds(first, 8), :]
        for k in range(8):
            out_ref[pl.ds(target_ref[first + k], 1), :] = block[k:k + 1, :]
        return carry

    lax.fori_loop(0, rows_ref.shape[0] // 8, body, 0, unroll=2)


def gather_kernel(source_ref, rows_ref, out_ref):
    def body(block, carry):
        first = pl.multiple_of(block * 128, 128)
        parts = [rows_ref[pl.ds(source_ref[first + k], 1), :] for k in range(128)]
        out_ref[:, pl.ds(first, 128)] = jnp.concatenate(parts, axis=0).T
        return carry

    lax.fori_loop(0, out_ref.shape[1] // 128, body, 0)


def scatter_rows(target, rows, slots):
    return pl.pallas_call(
        scatter_kernel,
        out_shape=jax.ShapeDtypeStruct((slots, rows.shape[1]), rows.dtype),
        in_specs=[pl.BlockSpec(memory_space=pltpu.SMEM), pl.BlockSpec(memory_space=pltpu.VMEM)],
        out_specs=pl.BlockSpec(memory_space=pltpu.VMEM),
    )(target, rows)


def gather_rows(source, rows):
    return pl.pallas_call(
        gather_kernel,
        out_shape=jax.ShapeDtypeStruct((rows.shape[1], source.shape[0]), rows.dtype),
        in_specs=[pl.BlockSpec(memory_space=pltpu.SMEM), pl.BlockSpec(memory_space=pltpu.VMEM)],
        out_specs=pl.BlockSpec(memory_space=pltpu.VMEM),
    )(source, rows)


def flat_chunks(rows, devices):
    slots, width = rows.shape
    chunk = slots // devices * width
    padded = -(-chunk // 1024) * 1024
    flat = jnp.pad(rows.reshape(devices, chunk), ((0, 0), (0, padded - chunk)))
    return flat.reshape(devices, padded // 128, 128)


def exchange_chunks(flat, slots, width):
    devices = flat.shape[0]
    chunk = slots // devices * width
    arrived = lax.all_to_all(flat, ("band", "lon"), 0, 0, tiled=True)
    return arrived.reshape(devices, -1)[:, :chunk].reshape(slots, width)


def slot_of(tiles, devices, block_rows):
    count = tiles.shape[0]
    blocks = count // block_rows
    one_hot = (tiles[:, None] == jnp.arange(devices, dtype=jnp.int32)[None, :]).astype(jnp.bfloat16)
    one_hot = one_hot.reshape(blocks, block_rows, devices)
    positions = jnp.arange(block_rows, dtype=jnp.int32)
    lower_tri = (positions[:, None] > positions[None, :]).astype(jnp.bfloat16)
    within = jnp.einsum("ab,kbt->kat", lower_tri, one_hot, preferred_element_type=jnp.float32)
    totals = jnp.sum(one_hot.astype(jnp.float32), axis=1)
    offsets = jnp.cumsum(totals, axis=0) - totals
    before = within + offsets[:, None, :]
    rank = jnp.sum(before * one_hot.astype(jnp.float32), axis=2)
    return rank.reshape(count).astype(jnp.int32)


def on_device(
    control,
    background_std,
    diffusivity,
    land_sea,
    departures,
    obs_frac,
    obs_weight,
    obs_cell,
    obs_tile,
):
    values = control.shape[0]
    tile_lat = control.shape[1]
    tile_lon = control.shape[2]
    band_count = lax.axis_size("band")
    lon_count = lax.axis_size("lon")
    devices = band_count * lon_count
    count = obs_tile.shape[0]
    block_rows = 512
    blocks = count // block_rows
    capacity = 5 * count // (4 * devices)
    slots = devices * capacity
    tiles = obs_tile[:, 0]
    target = tiles * capacity + slot_of(tiles, devices, block_rows)
    target = jnp.clip(target, 0, slots - 1)
    payload = jnp.concatenate(
        [departures, obs_frac, obs_weight[None, :], obs_cell.astype(jnp.float32)[None, :]], axis=0
    )
    outgoing = flat_chunks(scatter_rows(target, payload.T, slots), devices)
    outgoing, control, diffusivity, land_sea = lax.optimization_barrier(
        (outgoing, control, diffusivity, land_sea)
    )
    sea = land_sea.astype(jnp.float32)
    depth = PASSES
    stacked = jnp.concatenate([control * sea[None], diffusivity[None], sea[None]], axis=0)
    rimmed = with_halo(stacked, depth)
    lat_rows = (
        lax.axis_index("band") * tile_lat
        - depth
        + jnp.arange(tile_lat + 2 * depth, dtype=jnp.int32)
    )
    inside = ((lat_rows >= 0) & (lat_rows < band_count * tile_lat)).astype(jnp.float32)
    south, east = face_weights(rimmed[values], rimmed[values + 1] * inside[:, None])
    state = smooth_padded(rimmed[:values], south, east)
    increment = state * background_std[:, None, None]
    arrived = exchange_chunks(outgoing, slots, values + 4).T
    depart = arrived[:values]
    lat_frac = arrived[values]
    lon_frac = arrived[values + 1]
    row_weight = arrived[values + 2]
    cell = arrived[values + 3].astype(jnp.int32)
    lat_start = cell // (tile_lon - 1)
    lon_start = cell % (tile_lon - 1)
    lat_ids = jnp.arange(tile_lat, dtype=jnp.int32)[:, None]
    lon_ids = jnp.arange(tile_lon, dtype=jnp.int32)[:, None]
    lat_table = (lat_ids == lat_start[None, :]).astype(jnp.float32) * (1.0 - lat_frac)[None, :]
    lat_table = (
        lat_table + (lat_ids == lat_start[None, :] + 1).astype(jnp.float32) * lat_frac[None, :]
    )
    lon_table = (lon_ids == lon_start[None, :]).astype(jnp.float32) * (1.0 - lon_frac)[None, :]
    lon_table = (
        lon_table + (lon_ids == lon_start[None, :] + 1).astype(jnp.float32) * lon_frac[None, :]
    )
    partial_rows = jnp.einsum(
        "vij,jn->vin", increment, lon_table, precision=HIGH, preferred_element_type=jnp.float32
    )
    equiv = jnp.sum(partial_rows * lat_table[None, :, :], axis=1)
    misfit = row_weight * (equiv - depart)
    back = flat_chunks(misfit.T, devices)
    back, misfit = lax.optimization_barrier((back, misfit))
    spread = misfit[:, None, :] * lat_table[None, :, :]
    adjoint = jnp.einsum(
        "vin,jn->vij", spread, lon_table, precision=HIGH, preferred_element_type=jnp.float32
    )
    adjoint = adjoint * background_std[:, None, None]
    gradient = control + sea[None] * smooth(adjoint, south, east)
    returned = exchange_chunks(back, slots, values)
    obs_residual = gather_rows(target, returned)
    return (gradient, obs_residual)


def solution(mesh):
    in_specs = (
        P(None, "band", "lon"),
        P(),
        P("band", "lon"),
        P("band", "lon"),
        P(None, ("band", "lon")),
        P(None, ("band", "lon")),
        P(("band", "lon")),
        P(("band", "lon")),
        P(("band", "lon"), None),
    )
    out_specs = (P(None, "band", "lon"), P(None, ("band", "lon")))
    return jax.shard_map(
        on_device, mesh=mesh, in_specs=in_specs, out_specs=out_specs, check_vma=False
    )
```

```python
import jax
import jax.numpy as jnp
from jax import lax
from jax.experimental import pallas as pl
from jax.experimental.pallas import tpu as pltpu
from jax.sharding import PartitionSpec as P

PASSES = 4


HIGH = lax.Precision.HIGH


def ring_halo(array, axis, dim, width):
    count, length = (lax.axis_size(axis), array.shape[dim])
    up = [(i, (i + 1) % count) for i in range(count)]
    down = [(j, i) for i, j in up]
    last = lax.slice_in_dim(array, length - width, length, axis=dim)
    initial = lax.slice_in_dim(array, 0, width, axis=dim)
    before = lax.ppermute(last, axis, up)
    after = lax.ppermute(initial, axis, down)
    return jnp.concatenate([before, array, after], axis=dim)


def with_halo(array, width):
    array = ring_halo(array, "band", array.ndim - 2, width)
    return ring_halo(array, "lon", array.ndim - 1, width)


def face_weights(kappa_pad, sea_pad):
    south = 0.5 * (kappa_pad[:-1, :] + kappa_pad[1:, :]) * sea_pad[:-1, :] * sea_pad[1:, :]
    east = 0.5 * (kappa_pad[:, :-1] + kappa_pad[:, 1:]) * sea_pad[:, :-1] * sea_pad[:, 1:]
    return (south, east)


def diffuse_once(field, south, east):
    flux_south = south * (field[:, 1:, :] - field[:, :-1, :])
    flux_east = east * (field[:, :, 1:] - field[:, :, :-1])
    zero_lat = ((0, 0), (0, 1), (0, 0))
    along_lat = jnp.pad(flux_south, zero_lat) - jnp.pad(flux_south, ((0, 0), (1, 0), (0, 0)))
    along_lon = jnp.pad(flux_east, ((0, 0), (0, 0), (0, 1))) - jnp.pad(flux_east, ((0, 0), (0, 0), (1, 0)))
    return field + along_lat + along_lon


def smooth_padded(result, south, east):
    tile_lat, tile_lon = result.shape[1] - 2 * PASSES, result.shape[2] - 2 * PASSES
    result = lax.fori_loop(0, PASSES, lambda step, field: diffuse_once(field, south, east), result)
    return result[:, PASSES:PASSES + tile_lat, PASSES:PASSES + tile_lon]


def smooth(field, south, east):
    return smooth_padded(with_halo(field, PASSES), south, east)


def scatter_kernel(target_ref, columns_ref, out_ref):
    out_ref[...] = jnp.zeros(out_ref.shape, out_ref.dtype)

    def body(block, carry):
        first = pl.multiple_of(block * 128, 128)
        rows = columns_ref[:, pl.ds(first, 128)].T
        for k in range(128):
            out_ref[pl.ds(target_ref[first + k], 1), :] = rows[k:k + 1, :]
        return carry

    lax.fori_loop(0, columns_ref.shape[1] // 128, body, 0)


def to_columns_kernel(in_ref, out_ref):
    def body(block, carry):
        first = pl.multiple_of(block * 128, 128)
        out_ref[:, pl.ds(first, 128)] = in_ref[pl.ds(first, 128), :].T
        return carry

    lax.fori_loop(0, in_ref.shape[0] // 128, body, 0)


def to_rows_kernel(in_ref, out_ref):
    def body(block, carry):
        first = pl.multiple_of(block * 128, 128)
        out_ref[pl.ds(first, 128), :] = in_ref[:, pl.ds(first, 128)].T
        return carry

    lax.fori_loop(0, in_ref.shape[1] // 128, body, 0)


def transposed(kernel, array):
    return pl.pallas_call(
        kernel,
        out_shape=jax.ShapeDtypeStruct(array.shape[::-1], array.dtype),
        in_specs=[pl.BlockSpec(memory_space=pltpu.VMEM)],
        out_specs=pl.BlockSpec(memory_space=pltpu.VMEM),
    )(array)


def gather_kernel(source_ref, rows_ref, out_ref):
    def body(block, carry):
        first = pl.multiple_of(block * 128, 128)
        parts = [rows_ref[pl.ds(source_ref[first + k], 1), :] for k in range(128)]
        out_ref[:, pl.ds(first, 128)] = jnp.concatenate(parts, axis=0).T
        return carry

    lax.fori_loop(0, out_ref.shape[1] // 128, body, 0)


def scatter_rows(target, columns, slots):
    return pl.pallas_call(
        scatter_kernel,
        out_shape=jax.ShapeDtypeStruct((slots, columns.shape[0]), columns.dtype),
        in_specs=[pl.BlockSpec(memory_space=pltpu.SMEM), pl.BlockSpec(memory_space=pltpu.VMEM)],
        out_specs=pl.BlockSpec(memory_space=pltpu.VMEM),
    )(target, columns)


def gather_rows(source, rows):
    return pl.pallas_call(
        gather_kernel,
        out_shape=jax.ShapeDtypeStruct((rows.shape[1], source.shape[0]), rows.dtype),
        in_specs=[pl.BlockSpec(memory_space=pltpu.SMEM), pl.BlockSpec(memory_space=pltpu.VMEM)],
        out_specs=pl.BlockSpec(memory_space=pltpu.VMEM),
    )(source, rows)


def flat_chunks(rows, devices):
    slots, width = rows.shape
    chunk = slots // devices * width
    padded = -(-chunk // 1024) * 1024
    flat = jnp.pad(rows.reshape(devices, chunk), ((0, 0), (0, padded - chunk)))
    return flat.reshape(devices, padded // 128, 128)


def exchange_chunks(flat, slots, width):
    devices = flat.shape[0]
    chunk = slots // devices * width
    arrived = lax.all_to_all(flat, ("band", "lon"), 0, 0, tiled=True)
    return arrived.reshape(devices, -1)[:, :chunk].reshape(slots, width)


def slot_of(tiles, devices, block_rows):
    count = tiles.shape[0]
    blocks = count // block_rows
    one_hot = (tiles[:, None] == jnp.arange(devices, dtype=jnp.int32)[None, :]).astype(jnp.bfloat16)
    one_hot = one_hot.reshape(blocks, block_rows, devices)
    positions = jnp.arange(block_rows, dtype=jnp.int32)
    lower_tri = (positions[:, None] > positions[None, :]).astype(jnp.bfloat16)
    within = jnp.einsum("ab,kbt->kat", lower_tri, one_hot, preferred_element_type=jnp.float32)
    totals = jnp.sum(one_hot.astype(jnp.float32), axis=1)
    offsets = jnp.cumsum(totals, axis=0) - totals
    before = within + offsets[:, None, :]
    rank = jnp.sum(before * one_hot.astype(jnp.float32), axis=2)
    return rank.reshape(count).astype(jnp.int32)


def on_device(
    control,
    background_std,
    diffusivity,
    land_sea,
    departures,
    obs_frac,
    obs_weight,
    obs_cell,
    obs_tile,
):
    values = control.shape[0]
    tile_lat = control.shape[1]
    tile_lon = control.shape[2]
    band_count = lax.axis_size("band")
    lon_count = lax.axis_size("lon")
    devices = band_count * lon_count
    count = obs_tile.shape[0]
    block_rows = 512
    blocks = count // block_rows
    capacity = 5 * count // (4 * devices)
    slots = devices * capacity
    tiles = obs_tile[:, 0]
    target = tiles * capacity + slot_of(tiles, devices, block_rows)
    target = jnp.clip(target, 0, slots - 1)
    payload = jnp.concatenate(
        [departures, obs_frac, obs_weight[None, :], obs_cell.astype(jnp.float32)[None, :]], axis=0
    )
    outgoing = flat_chunks(scatter_rows(target, payload, slots), devices)
    outgoing, control, diffusivity, land_sea = lax.optimization_barrier(
        (outgoing, control, diffusivity, land_sea)
    )
    sea = land_sea.astype(jnp.float32)
    depth = PASSES
    stacked = jnp.concatenate([control * sea[None], diffusivity[None], sea[None]], axis=0)
    rimmed = with_halo(stacked, depth)
    lat_rows = (
        lax.axis_index("band") * tile_lat
        - depth
        + jnp.arange(tile_lat + 2 * depth, dtype=jnp.int32)
    )
    inside = ((lat_rows >= 0) & (lat_rows < band_count * tile_lat)).astype(jnp.float32)
    south, east = face_weights(rimmed[values], rimmed[values + 1] * inside[:, None])
    state = smooth_padded(rimmed[:values], south, east)
    increment = state * background_std[:, None, None]
    arrived = transposed(to_columns_kernel, exchange_chunks(outgoing, slots, values + 4))
    depart = arrived[:values]
    lat_frac = arrived[values]
    lon_frac = arrived[values + 1]
    row_weight = arrived[values + 2]
    cell = arrived[values + 3].astype(jnp.int32)
    lat_start = cell // (tile_lon - 1)
    lon_start = cell % (tile_lon - 1)
    lat_ids = jnp.arange(tile_lat, dtype=jnp.int32)[:, None]
    lon_ids = jnp.arange(tile_lon, dtype=jnp.int32)[:, None]
    lat_table = (lat_ids == lat_start[None, :]).astype(jnp.float32) * (1.0 - lat_frac)[None, :]
    lat_table = (
        lat_table + (lat_ids == lat_start[None, :] + 1).astype(jnp.float32) * lat_frac[None, :]
    )
    lon_table = (lon_ids == lon_start[None, :]).astype(jnp.float32) * (1.0 - lon_frac)[None, :]
    lon_table = (
        lon_table + (lon_ids == lon_start[None, :] + 1).astype(jnp.float32) * lon_frac[None, :]
    )
    partial_rows = jnp.einsum(
        "vij,jn->vin", increment, lon_table, precision=HIGH, preferred_element_type=jnp.float32
    )
    equiv = jnp.sum(partial_rows * lat_table[None, :, :], axis=1)
    misfit = row_weight * (equiv - depart)
    back = flat_chunks(transposed(to_rows_kernel, misfit), devices)
    back, misfit = lax.optimization_barrier((back, misfit))
    spread = misfit[:, None, :] * lat_table[None, :, :]
    adjoint = jnp.einsum(
        "vin,jn->vij", spread, lon_table, precision=HIGH, preferred_element_type=jnp.float32
    )
    adjoint = adjoint * background_std[:, None, None]
    gradient = control + sea[None] * smooth(adjoint, south, east)
    returned = exchange_chunks(back, slots, values)
    obs_residual = gather_rows(target, returned)
    return (gradient, obs_residual)


def solution(mesh):
    in_specs = (
        P(None, "band", "lon"),
        P(),
        P("band", "lon"),
        P("band", "lon"),
        P(None, ("band", "lon")),
        P(None, ("band", "lon")),
        P(("band", "lon")),
        P(("band", "lon")),
        P(("band", "lon"), None),
    )
    out_specs = (P(None, "band", "lon"), P(None, ("band", "lon")))
    return jax.shard_map(
        on_device, mesh=mesh, in_specs=in_specs, out_specs=out_specs, check_vma=False
    )
```

```python
import jax
import jax.numpy as jnp
from jax import lax
from jax.experimental import pallas as pl
from jax.experimental.pallas import tpu as pltpu
from jax.sharding import PartitionSpec as P

PASSES = 4


HIGH = lax.Precision.HIGH


def ring_halo(array, axis, dim, width):
    count, length = (lax.axis_size(axis), array.shape[dim])
    up = [(i, (i + 1) % count) for i in range(count)]
    down = [(j, i) for i, j in up]
    last = lax.slice_in_dim(array, length - width, length, axis=dim)
    initial = lax.slice_in_dim(array, 0, width, axis=dim)
    before = lax.ppermute(last, axis, up)
    after = lax.ppermute(initial, axis, down)
    return jnp.concatenate([before, array, after], axis=dim)


def with_halo(array, width):
    array = ring_halo(array, "band", array.ndim - 2, width)
    return ring_halo(array, "lon", array.ndim - 1, width)


def face_weights(kappa_pad, sea_pad):
    south = 0.5 * (kappa_pad[:-1, :] + kappa_pad[1:, :]) * sea_pad[:-1, :] * sea_pad[1:, :]
    east = 0.5 * (kappa_pad[:, :-1] + kappa_pad[:, 1:]) * sea_pad[:, :-1] * sea_pad[:, 1:]
    return (south, east)


def diffuse_once(field, south, east):
    flux_south = south * (field[:, 1:, :] - field[:, :-1, :])
    flux_east = east * (field[:, :, 1:] - field[:, :, :-1])
    zero_lat = ((0, 0), (0, 1), (0, 0))
    along_lat = jnp.pad(flux_south, zero_lat) - jnp.pad(flux_south, ((0, 0), (1, 0), (0, 0)))
    along_lon = jnp.pad(flux_east, ((0, 0), (0, 0), (0, 1))) - jnp.pad(flux_east, ((0, 0), (0, 0), (1, 0)))
    return field + along_lat + along_lon


def smooth_padded(result, south, east):
    tile_lat, tile_lon = result.shape[1] - 2 * PASSES, result.shape[2] - 2 * PASSES
    result = lax.fori_loop(0, PASSES, lambda step, field: diffuse_once(field, south, east), result)
    return result[:, PASSES:PASSES + tile_lat, PASSES:PASSES + tile_lon]


def smooth(field, south, east):
    return smooth_padded(with_halo(field, PASSES), south, east)


def scatter_kernel(target_ref, rows_ref, out_ref):
    out_ref[...] = jnp.zeros(out_ref.shape, out_ref.dtype)

    def body(group, carry):
        first = pl.multiple_of(group * 8, 8)
        block = rows_ref[pl.ds(first, 8), :]
        for k in range(8):
            out_ref[pl.ds(target_ref[first + k], 1), :] = block[k:k + 1, :]
        return carry

    lax.fori_loop(0, rows_ref.shape[0] // 8, body, 0, unroll=2)


def gather_kernel(source_ref, rows_ref, out_ref):
    def body(block, carry):
        first = pl.multiple_of(block * 128, 128)
        parts = [rows_ref[pl.ds(source_ref[first + k], 1), :] for k in range(128)]
        out_ref[:, pl.ds(first, 128)] = jnp.concatenate(parts, axis=0).T
        return carry

    lax.fori_loop(0, out_ref.shape[1] // 128, body, 0)


def scatter_rows(target, rows, slots):
    return pl.pallas_call(
        scatter_kernel,
        out_shape=jax.ShapeDtypeStruct((slots, rows.shape[1]), rows.dtype),
        in_specs=[pl.BlockSpec(memory_space=pltpu.SMEM), pl.BlockSpec(memory_space=pltpu.VMEM)],
        out_specs=pl.BlockSpec(memory_space=pltpu.VMEM),
    )(target, rows)


def gather_rows(source, rows):
    return pl.pallas_call(
        gather_kernel,
        out_shape=jax.ShapeDtypeStruct((rows.shape[1], source.shape[0]), rows.dtype),
        in_specs=[pl.BlockSpec(memory_space=pltpu.SMEM), pl.BlockSpec(memory_space=pltpu.VMEM)],
        out_specs=pl.BlockSpec(memory_space=pltpu.VMEM),
    )(source, rows)


def flat_chunks(rows, devices):
    slots, width = rows.shape
    chunk = slots // devices * width
    padded = -(-chunk // 1024) * 1024
    flat = jnp.pad(rows.reshape(devices, chunk), ((0, 0), (0, padded - chunk)))
    return flat.reshape(devices, padded // 128, 128)


def exchange_chunks(flat, slots, width):
    devices = flat.shape[0]
    chunk = slots // devices * width
    arrived = lax.all_to_all(flat, ("band", "lon"), 0, 0, tiled=True)
    return arrived.reshape(devices, -1)[:, :chunk].reshape(slots, width)


def slot_of(tiles, devices, block_rows):
    count = tiles.shape[0]
    blocks = count // block_rows
    one_hot = (tiles[:, None] == jnp.arange(devices, dtype=jnp.int32)[None, :]).astype(jnp.bfloat16)
    one_hot = one_hot.reshape(blocks, block_rows, devices)
    positions = jnp.arange(block_rows, dtype=jnp.int32)
    lower_tri = (positions[:, None] > positions[None, :]).astype(jnp.bfloat16)
    within = jnp.einsum("ab,kbt->kat", lower_tri, one_hot, preferred_element_type=jnp.float32)
    totals = jnp.sum(one_hot.astype(jnp.float32), axis=1)
    offsets = jnp.cumsum(totals, axis=0) - totals
    before = within + offsets[:, None, :]
    rank = jnp.sum(before * one_hot.astype(jnp.float32), axis=2)
    return rank.reshape(count).astype(jnp.int32)


def on_device(
    control,
    background_std,
    diffusivity,
    land_sea,
    departures,
    obs_frac,
    obs_weight,
    obs_cell,
    obs_tile,
):
    values = control.shape[0]
    tile_lat = control.shape[1]
    tile_lon = control.shape[2]
    band_count = lax.axis_size("band")
    lon_count = lax.axis_size("lon")
    devices = band_count * lon_count
    count = obs_tile.shape[0]
    block_rows = 512
    blocks = count // block_rows
    capacity = 5 * count // (4 * devices)
    slots = devices * capacity
    tiles = obs_tile[:, 0]
    target = tiles * capacity + slot_of(tiles, devices, block_rows)
    target = jnp.clip(target, 0, slots - 1)
    payload = jnp.concatenate(
        [departures, obs_frac, obs_weight[None, :], obs_cell.astype(jnp.float32)[None, :]], axis=0
    )
    outgoing = flat_chunks(scatter_rows(target, payload.T, slots), devices)
    outgoing, control, diffusivity, land_sea = lax.optimization_barrier(
        (outgoing, control, diffusivity, land_sea)
    )
    sea = land_sea.astype(jnp.float32)
    depth = PASSES
    stacked = jnp.concatenate([control * sea[None], diffusivity[None], sea[None]], axis=0)
    rimmed = with_halo(stacked, depth)
    lat_rows = (
        lax.axis_index("band") * tile_lat
        - depth
        + jnp.arange(tile_lat + 2 * depth, dtype=jnp.int32)
    )
    inside = ((lat_rows >= 0) & (lat_rows < band_count * tile_lat)).astype(jnp.float32)
    south, east = face_weights(rimmed[values], rimmed[values + 1] * inside[:, None])
    state = smooth_padded(rimmed[:values], south, east)
    increment = state * background_std[:, None, None]
    arrived = exchange_chunks(outgoing, slots, values + 4).T
    depart = arrived[:values]
    lat_frac = arrived[values]
    lon_frac = arrived[values + 1]
    row_weight = arrived[values + 2]
    cell = arrived[values + 3].astype(jnp.int32)
    lat_start = cell // (tile_lon - 1)
    lon_start = cell % (tile_lon - 1)
    lat_ids = jnp.arange(tile_lat, dtype=jnp.int32)[:, None]
    lon_ids = jnp.arange(tile_lon, dtype=jnp.int32)[:, None]
    lat_table = (lat_ids == lat_start[None, :]).astype(jnp.float32) * (1.0 - lat_frac)[None, :]
    lat_table = (
        lat_table + (lat_ids == lat_start[None, :] + 1).astype(jnp.float32) * lat_frac[None, :]
    )
    lon_table = (lon_ids == lon_start[None, :]).astype(jnp.float32) * (1.0 - lon_frac)[None, :]
    lon_table = (
        lon_table + (lon_ids == lon_start[None, :] + 1).astype(jnp.float32) * lon_frac[None, :]
    )
    partial_rows = jnp.einsum(
        "vij,jn->vin", increment, lon_table, precision=HIGH, preferred_element_type=jnp.float32
    )
    equiv = jnp.sum(partial_rows * lat_table[None, :, :], axis=1)
    misfit = row_weight * (equiv - depart)
    split = values // 2
    back_first = flat_chunks(misfit[:split].T, devices)
    back_second = flat_chunks(misfit[split:].T, devices)
    back_first, back_second, misfit = lax.optimization_barrier((back_first, back_second, misfit))
    spread = misfit[:, None, :] * lat_table[None, :, :]
    adjoint = jnp.einsum(
        "vin,jn->vij", spread, lon_table, precision=HIGH, preferred_element_type=jnp.float32
    )
    adjoint = adjoint * background_std[:, None, None]
    gradient = control + sea[None] * smooth(adjoint, south, east)
    returned = jnp.concatenate(
        [
            exchange_chunks(back_first, slots, split),
            exchange_chunks(back_second, slots, values - split),
        ],
        axis=1,
    )
    obs_residual = gather_rows(target, returned)
    return (gradient, obs_residual)


def solution(mesh):
    in_specs = (
        P(None, "band", "lon"),
        P(),
        P("band", "lon"),
        P("band", "lon"),
        P(None, ("band", "lon")),
        P(None, ("band", "lon")),
        P(("band", "lon")),
        P(("band", "lon")),
        P(("band", "lon"), None),
    )
    out_specs = (P(None, "band", "lon"), P(None, ("band", "lon")))
    return jax.shard_map(
        on_device, mesh=mesh, in_specs=in_specs, out_specs=out_specs, check_vma=False
    )
```

```python
import jax
import jax.numpy as jnp
from jax import lax
from jax.experimental import pallas as pl
from jax.experimental.pallas import tpu as pltpu
from jax.sharding import PartitionSpec as P

PASSES = 4


HIGH = lax.Precision.HIGH


def ring_halo(array, axis, dim, width):
    count, length = (lax.axis_size(axis), array.shape[dim])
    up = [(i, (i + 1) % count) for i in range(count)]
    down = [(j, i) for i, j in up]
    last = lax.slice_in_dim(array, length - width, length, axis=dim)
    initial = lax.slice_in_dim(array, 0, width, axis=dim)
    before = lax.ppermute(last, axis, up)
    after = lax.ppermute(initial, axis, down)
    return jnp.concatenate([before, array, after], axis=dim)


def with_halo(array, width):
    array = ring_halo(array, "band", array.ndim - 2, width)
    return ring_halo(array, "lon", array.ndim - 1, width)


def face_weights(kappa_pad, sea_pad):
    south = 0.5 * (kappa_pad[:-1, :] + kappa_pad[1:, :]) * sea_pad[:-1, :] * sea_pad[1:, :]
    east = 0.5 * (kappa_pad[:, :-1] + kappa_pad[:, 1:]) * sea_pad[:, :-1] * sea_pad[:, 1:]
    return (south, east)


def diffuse_once(field, south, east):
    flux_south = south * (field[:, 1:, :] - field[:, :-1, :])
    flux_east = east * (field[:, :, 1:] - field[:, :, :-1])
    zero_lat = ((0, 0), (0, 1), (0, 0))
    along_lat = jnp.pad(flux_south, zero_lat) - jnp.pad(flux_south, ((0, 0), (1, 0), (0, 0)))
    along_lon = jnp.pad(flux_east, ((0, 0), (0, 0), (0, 1))) - jnp.pad(flux_east, ((0, 0), (0, 0), (1, 0)))
    return field + along_lat + along_lon


def smooth_padded(result, south, east):
    tile_lat, tile_lon = result.shape[1] - 2 * PASSES, result.shape[2] - 2 * PASSES
    result = lax.fori_loop(0, PASSES, lambda step, field: diffuse_once(field, south, east), result)
    return result[:, PASSES:PASSES + tile_lat, PASSES:PASSES + tile_lon]


def smooth(field, south, east):
    return smooth_padded(with_halo(field, PASSES), south, east)


def scatter_kernel(target_ref, columns_ref, out_ref):
    out_ref[...] = jnp.zeros(out_ref.shape, out_ref.dtype)

    def body(block, carry):
        first = pl.multiple_of(block * 128, 128)
        rows = columns_ref[:, pl.ds(first, 128)].T
        for k in range(128):
            out_ref[pl.ds(target_ref[first + k], 1), :] = rows[k:k + 1, :]
        return carry

    lax.fori_loop(0, columns_ref.shape[1] // 128, body, 0)


def gather_kernel(source_ref, rows_ref, out_ref):
    def body(block, carry):
        first = pl.multiple_of(block * 128, 128)
        parts = [rows_ref[pl.ds(source_ref[first + k], 1), :] for k in range(128)]
        out_ref[:, pl.ds(first, 128)] = jnp.concatenate(parts, axis=0).T
        return carry

    lax.fori_loop(0, out_ref.shape[1] // 128, body, 0)


def scatter_rows(target, columns, slots):
    return pl.pallas_call(
        scatter_kernel,
        out_shape=jax.ShapeDtypeStruct((slots, columns.shape[0]), columns.dtype),
        in_specs=[pl.BlockSpec(memory_space=pltpu.SMEM), pl.BlockSpec(memory_space=pltpu.VMEM)],
        out_specs=pl.BlockSpec(memory_space=pltpu.VMEM),
    )(target, columns)


def gather_rows(source, rows):
    return pl.pallas_call(
        gather_kernel,
        out_shape=jax.ShapeDtypeStruct((rows.shape[1], source.shape[0]), rows.dtype),
        in_specs=[pl.BlockSpec(memory_space=pltpu.SMEM), pl.BlockSpec(memory_space=pltpu.VMEM)],
        out_specs=pl.BlockSpec(memory_space=pltpu.VMEM),
    )(source, rows)


def flat_chunks(rows, devices):
    slots, width = rows.shape
    chunk = slots // devices * width
    padded = -(-chunk // 1024) * 1024
    flat = jnp.pad(rows.reshape(devices, chunk), ((0, 0), (0, padded - chunk)))
    return flat.reshape(devices, padded // 128, 128)


def exchange_chunks(flat, slots, width):
    devices = flat.shape[0]
    chunk = slots // devices * width
    arrived = lax.all_to_all(flat, ("band", "lon"), 0, 0, tiled=True)
    return arrived.reshape(devices, -1)[:, :chunk].reshape(slots, width)


def slot_of(tiles, devices, block_rows):
    count = tiles.shape[0]
    blocks = count // block_rows
    one_hot = (tiles[:, None] == jnp.arange(devices, dtype=jnp.int32)[None, :]).astype(jnp.bfloat16)
    one_hot = one_hot.reshape(blocks, block_rows, devices)
    positions = jnp.arange(block_rows, dtype=jnp.int32)
    lower_tri = (positions[:, None] > positions[None, :]).astype(jnp.bfloat16)
    within = jnp.einsum("ab,kbt->kat", lower_tri, one_hot, preferred_element_type=jnp.float32)
    totals = jnp.sum(one_hot.astype(jnp.float32), axis=1)
    offsets = jnp.cumsum(totals, axis=0) - totals
    before = within + offsets[:, None, :]
    rank = jnp.sum(before * one_hot.astype(jnp.float32), axis=2)
    return rank.reshape(count).astype(jnp.int32)


def on_device(
    control,
    background_std,
    diffusivity,
    land_sea,
    departures,
    obs_frac,
    obs_weight,
    obs_cell,
    obs_tile,
):
    values = control.shape[0]
    tile_lat = control.shape[1]
    tile_lon = control.shape[2]
    band_count = lax.axis_size("band")
    lon_count = lax.axis_size("lon")
    devices = band_count * lon_count
    count = obs_tile.shape[0]
    block_rows = 512
    blocks = count // block_rows
    capacity = 5 * count // (4 * devices)
    slots = devices * capacity
    tiles = obs_tile[:, 0]
    target = tiles * capacity + slot_of(tiles, devices, block_rows)
    target = jnp.clip(target, 0, slots - 1)
    payload = jnp.concatenate(
        [departures, obs_frac, obs_weight[None, :], obs_cell.astype(jnp.float32)[None, :]], axis=0
    )
    outgoing = flat_chunks(scatter_rows(target, payload, slots), devices)
    outgoing, control, diffusivity, land_sea = lax.optimization_barrier(
        (outgoing, control, diffusivity, land_sea)
    )
    sea = land_sea.astype(jnp.float32)
    depth = PASSES
    stacked = jnp.concatenate([control * sea[None], diffusivity[None], sea[None]], axis=0)
    rimmed = with_halo(stacked, depth)
    lat_rows = (
        lax.axis_index("band") * tile_lat
        - depth
        + jnp.arange(tile_lat + 2 * depth, dtype=jnp.int32)
    )
    inside = ((lat_rows >= 0) & (lat_rows < band_count * tile_lat)).astype(jnp.float32)
    south, east = face_weights(rimmed[values], rimmed[values + 1] * inside[:, None])
    state = smooth_padded(rimmed[:values], south, east)
    increment = state * background_std[:, None, None]
    arrived = exchange_chunks(outgoing, slots, values + 4).T
    depart = arrived[:values]
    lat_frac = arrived[values]
    lon_frac = arrived[values + 1]
    row_weight = arrived[values + 2]
    cell = arrived[values + 3].astype(jnp.int32)
    lat_start = cell // (tile_lon - 1)
    lon_start = cell % (tile_lon - 1)
    lat_ids = jnp.arange(tile_lat, dtype=jnp.int32)[:, None]
    lon_ids = jnp.arange(tile_lon, dtype=jnp.int32)[:, None]
    lat_table = (lat_ids == lat_start[None, :]).astype(jnp.float32) * (1.0 - lat_frac)[None, :]
    lat_table = (
        lat_table + (lat_ids == lat_start[None, :] + 1).astype(jnp.float32) * lat_frac[None, :]
    )
    lon_table = (lon_ids == lon_start[None, :]).astype(jnp.float32) * (1.0 - lon_frac)[None, :]
    lon_table = (
        lon_table + (lon_ids == lon_start[None, :] + 1).astype(jnp.float32) * lon_frac[None, :]
    )
    partial_rows = jnp.einsum(
        "vij,jn->vin", increment, lon_table, precision=HIGH, preferred_element_type=jnp.float32
    )
    equiv = jnp.sum(partial_rows * lat_table[None, :, :], axis=1)
    misfit = row_weight * (equiv - depart)
    back = flat_chunks(misfit.T, devices)
    back, misfit = lax.optimization_barrier((back, misfit))
    spread = misfit[:, None, :] * lat_table[None, :, :]
    adjoint = jnp.einsum(
        "vin,jn->vij", spread, lon_table, precision=HIGH, preferred_element_type=jnp.float32
    )
    adjoint = adjoint * background_std[:, None, None]
    gradient = control + sea[None] * smooth(adjoint, south, east)
    returned = exchange_chunks(back, slots, values)
    obs_residual = gather_rows(target, returned)
    return (gradient, obs_residual)


def solution(mesh):
    in_specs = (
        P(None, "band", "lon"),
        P(),
        P("band", "lon"),
        P("band", "lon"),
        P(None, ("band", "lon")),
        P(None, ("band", "lon")),
        P(("band", "lon")),
        P(("band", "lon")),
        P(("band", "lon"), None),
    )
    out_specs = (P(None, "band", "lon"), P(None, ("band", "lon")))
    return jax.shard_map(
        on_device, mesh=mesh, in_specs=in_specs, out_specs=out_specs, check_vma=False
    )
```

```python
import jax
import jax.numpy as jnp
from jax import lax
from jax.experimental import pallas as pl
from jax.experimental.pallas import tpu as pltpu
from jax.sharding import PartitionSpec as P

PASSES = 4


HIGH = lax.Precision.HIGH


def ring_halo(array, axis, dim, width):
    count, length = (lax.axis_size(axis), array.shape[dim])
    up = [(i, (i + 1) % count) for i in range(count)]
    down = [(j, i) for i, j in up]
    last = lax.slice_in_dim(array, length - width, length, axis=dim)
    initial = lax.slice_in_dim(array, 0, width, axis=dim)
    before = lax.ppermute(last, axis, up)
    after = lax.ppermute(initial, axis, down)
    return jnp.concatenate([before, array, after], axis=dim)


def with_halo(array, width):
    array = ring_halo(array, "band", array.ndim - 2, width)
    return ring_halo(array, "lon", array.ndim - 1, width)


def face_weights(kappa_pad, sea_pad):
    south = 0.5 * (kappa_pad[:-1, :] + kappa_pad[1:, :]) * sea_pad[:-1, :] * sea_pad[1:, :]
    east = 0.5 * (kappa_pad[:, :-1] + kappa_pad[:, 1:]) * sea_pad[:, :-1] * sea_pad[:, 1:]
    return (south, east)


def diffuse_once(field, south, east):
    flux_south = south * (field[:, 1:, :] - field[:, :-1, :])
    flux_east = east * (field[:, :, 1:] - field[:, :, :-1])
    zero_lat = ((0, 0), (0, 1), (0, 0))
    along_lat = jnp.pad(flux_south, zero_lat) - jnp.pad(flux_south, ((0, 0), (1, 0), (0, 0)))
    along_lon = jnp.pad(flux_east, ((0, 0), (0, 0), (0, 1))) - jnp.pad(flux_east, ((0, 0), (0, 0), (1, 0)))
    return field + along_lat + along_lon


def smooth_padded(result, south, east):
    tile_lat, tile_lon = result.shape[1] - 2 * PASSES, result.shape[2] - 2 * PASSES
    result = lax.fori_loop(0, PASSES, lambda step, field: diffuse_once(field, south, east), result)
    return result[:, PASSES:PASSES + tile_lat, PASSES:PASSES + tile_lon]


def smooth(field, south, east):
    return smooth_padded(with_halo(field, PASSES), south, east)


def scatter_kernel(target_ref, columns_ref, out_ref):
    out_ref[...] = jnp.zeros(out_ref.shape, out_ref.dtype)

    def body(block, carry):
        first = pl.multiple_of(block * 128, 128)
        rows = columns_ref[:, pl.ds(first, 128)].T
        for k in range(128):
            out_ref[pl.ds(target_ref[first + k], 1), :] = rows[k:k + 1, :]
        return carry

    lax.fori_loop(0, columns_ref.shape[1] // 128, body, 0)


def gather_kernel(source_ref, rows_ref, out_ref):
    def body(block, carry):
        first = pl.multiple_of(block * 128, 128)
        parts = [rows_ref[pl.ds(source_ref[first + k], 1), :] for k in range(128)]
        out_ref[:, pl.ds(first, 128)] = jnp.concatenate(parts, axis=0).T
        return carry

    lax.fori_loop(0, out_ref.shape[1] // 128, body, 0)


def scatter_rows(target, columns, slots):
    return pl.pallas_call(
        scatter_kernel,
        out_shape=jax.ShapeDtypeStruct((slots, columns.shape[0]), columns.dtype),
        in_specs=[pl.BlockSpec(memory_space=pltpu.SMEM), pl.BlockSpec(memory_space=pltpu.VMEM)],
        out_specs=pl.BlockSpec(memory_space=pltpu.VMEM),
    )(target, columns)


def gather_rows(source, rows):
    return pl.pallas_call(
        gather_kernel,
        out_shape=jax.ShapeDtypeStruct((rows.shape[1], source.shape[0]), rows.dtype),
        in_specs=[pl.BlockSpec(memory_space=pltpu.SMEM), pl.BlockSpec(memory_space=pltpu.VMEM)],
        out_specs=pl.BlockSpec(memory_space=pltpu.VMEM),
    )(source, rows)


def flat_chunks(rows, devices):
    slots, width = rows.shape
    chunk = slots // devices * width
    padded = -(-chunk // 1024) * 1024
    flat = jnp.pad(rows.reshape(devices, chunk), ((0, 0), (0, padded - chunk)))
    return flat.reshape(devices, padded // 128, 128)


def exchange_chunks(flat, slots, width):
    devices = flat.shape[0]
    chunk = slots // devices * width
    arrived = lax.all_to_all(flat, ("band", "lon"), 0, 0, tiled=True)
    return arrived.reshape(devices, -1)[:, :chunk].reshape(slots, width)


def slot_of(tiles, devices, block_rows):
    count = tiles.shape[0]
    blocks = count // block_rows
    one_hot = (tiles[:, None] == jnp.arange(devices, dtype=jnp.int32)[None, :]).astype(jnp.bfloat16)
    one_hot = one_hot.reshape(blocks, block_rows, devices)
    positions = jnp.arange(block_rows, dtype=jnp.int32)
    lower_tri = (positions[:, None] > positions[None, :]).astype(jnp.bfloat16)
    within = jnp.einsum("ab,kbt->kat", lower_tri, one_hot, preferred_element_type=jnp.float32)
    totals = jnp.sum(one_hot.astype(jnp.float32), axis=1)
    offsets = jnp.cumsum(totals, axis=0) - totals
    before = within + offsets[:, None, :]
    rank = jnp.sum(before * one_hot.astype(jnp.float32), axis=2)
    return rank.reshape(count).astype(jnp.int32)


def on_device(
    control,
    background_std,
    diffusivity,
    land_sea,
    departures,
    obs_frac,
    obs_weight,
    obs_cell,
    obs_tile,
):
    values = control.shape[0]
    tile_lat = control.shape[1]
    tile_lon = control.shape[2]
    band_count = lax.axis_size("band")
    lon_count = lax.axis_size("lon")
    devices = band_count * lon_count
    count = obs_tile.shape[0]
    block_rows = 512
    blocks = count // block_rows
    capacity = 5 * count // (4 * devices)
    slots = devices * capacity
    tiles = obs_tile[:, 0]
    target = tiles * capacity + slot_of(tiles, devices, block_rows)
    target = jnp.clip(target, 0, slots - 1)
    payload = jnp.concatenate(
        [departures, obs_frac, obs_weight[None, :], obs_cell.astype(jnp.float32)[None, :]], axis=0
    )
    outgoing = flat_chunks(scatter_rows(target, payload, slots), devices)
    sea = land_sea.astype(jnp.float32)
    depth = PASSES
    stacked = jnp.concatenate([control * sea[None], diffusivity[None], sea[None]], axis=0)
    rimmed = with_halo(stacked, depth)
    lat_rows = (
        lax.axis_index("band") * tile_lat
        - depth
        + jnp.arange(tile_lat + 2 * depth, dtype=jnp.int32)
    )
    inside = ((lat_rows >= 0) & (lat_rows < band_count * tile_lat)).astype(jnp.float32)
    south, east = face_weights(rimmed[values], rimmed[values + 1] * inside[:, None])
    state = smooth_padded(rimmed[:values], south, east)
    increment = state * background_std[:, None, None]
    arrived = exchange_chunks(outgoing, slots, values + 4).T
    depart = arrived[:values]
    lat_frac = arrived[values]
    lon_frac = arrived[values + 1]
    row_weight = arrived[values + 2]
    cell = arrived[values + 3].astype(jnp.int32)
    lat_start = cell // (tile_lon - 1)
    lon_start = cell % (tile_lon - 1)
    lat_ids = jnp.arange(tile_lat, dtype=jnp.int32)[:, None]
    lon_ids = jnp.arange(tile_lon, dtype=jnp.int32)[:, None]
    lat_table = (lat_ids == lat_start[None, :]).astype(jnp.float32) * (1.0 - lat_frac)[None, :]
    lat_table = (
        lat_table + (lat_ids == lat_start[None, :] + 1).astype(jnp.float32) * lat_frac[None, :]
    )
    lon_table = (lon_ids == lon_start[None, :]).astype(jnp.float32) * (1.0 - lon_frac)[None, :]
    lon_table = (
        lon_table + (lon_ids == lon_start[None, :] + 1).astype(jnp.float32) * lon_frac[None, :]
    )
    partial_rows = jnp.einsum(
        "vij,jn->vin", increment, lon_table, precision=HIGH, preferred_element_type=jnp.float32
    )
    equiv = jnp.sum(partial_rows * lat_table[None, :, :], axis=1)
    misfit = row_weight * (equiv - depart)
    back = flat_chunks(misfit.T, devices)
    back, misfit = lax.optimization_barrier((back, misfit))
    spread = misfit[:, None, :] * lat_table[None, :, :]
    adjoint = jnp.einsum(
        "vin,jn->vij", spread, lon_table, precision=HIGH, preferred_element_type=jnp.float32
    )
    adjoint = adjoint * background_std[:, None, None]
    gradient = control + sea[None] * smooth(adjoint, south, east)
    returned = exchange_chunks(back, slots, values)
    obs_residual = gather_rows(target, returned)
    return (gradient, obs_residual)


def solution(mesh):
    in_specs = (
        P(None, "band", "lon"),
        P(),
        P("band", "lon"),
        P("band", "lon"),
        P(None, ("band", "lon")),
        P(None, ("band", "lon")),
        P(("band", "lon")),
        P(("band", "lon")),
        P(("band", "lon"), None),
    )
    out_specs = (P(None, "band", "lon"), P(None, ("band", "lon")))
    return jax.shard_map(
        on_device, mesh=mesh, in_specs=in_specs, out_specs=out_specs, check_vma=False
    )
```

```python
import jax
import jax.numpy as jnp
from jax import lax
from jax.experimental import pallas as pl
from jax.experimental.pallas import tpu as pltpu
from jax.sharding import PartitionSpec as P

PASSES = 4


HIGH = lax.Precision.HIGH


def ring_halo(array, axis, dim, width):
    count, length = (lax.axis_size(axis), array.shape[dim])
    up = [(i, (i + 1) % count) for i in range(count)]
    down = [(j, i) for i, j in up]
    last = lax.slice_in_dim(array, length - width, length, axis=dim)
    initial = lax.slice_in_dim(array, 0, width, axis=dim)
    before = lax.ppermute(last, axis, up)
    after = lax.ppermute(initial, axis, down)
    return jnp.concatenate([before, array, after], axis=dim)


def with_halo(array, width):
    array = ring_halo(array, "band", array.ndim - 2, width)
    return ring_halo(array, "lon", array.ndim - 1, width)


def face_weights(kappa_pad, sea_pad):
    south = 0.5 * (kappa_pad[:-1, :] + kappa_pad[1:, :]) * sea_pad[:-1, :] * sea_pad[1:, :]
    east = 0.5 * (kappa_pad[:, :-1] + kappa_pad[:, 1:]) * sea_pad[:, :-1] * sea_pad[:, 1:]
    return (south, east)


def diffuse_once(field, south, east):
    flux_south = south * (field[:, 1:, :] - field[:, :-1, :])
    flux_east = east * (field[:, :, 1:] - field[:, :, :-1])
    zero_lat = ((0, 0), (0, 1), (0, 0))
    along_lat = jnp.pad(flux_south, zero_lat) - jnp.pad(flux_south, ((0, 0), (1, 0), (0, 0)))
    along_lon = jnp.pad(flux_east, ((0, 0), (0, 0), (0, 1))) - jnp.pad(flux_east, ((0, 0), (0, 0), (1, 0)))
    return field + along_lat + along_lon


def smooth_padded(result, south, east):
    tile_lat, tile_lon = result.shape[1] - 2 * PASSES, result.shape[2] - 2 * PASSES
    result = lax.fori_loop(0, PASSES, lambda step, field: diffuse_once(field, south, east), result)
    return result[:, PASSES:PASSES + tile_lat, PASSES:PASSES + tile_lon]


def smooth(field, south, east):
    return smooth_padded(with_halo(field, PASSES), south, east)


def scatter_kernel(target_ref, columns_ref, out_ref):
    out_ref[...] = jnp.zeros(out_ref.shape, out_ref.dtype)

    def body(block, carry):
        first = pl.multiple_of(block * 128, 128)
        rows = columns_ref[:, pl.ds(first, 128)].T
        for k in range(128):
            out_ref[pl.ds(target_ref[first + k], 1), :] = rows[k:k + 1, :]
        return carry

    lax.fori_loop(0, columns_ref.shape[1] // 128, body, 0, unroll=2)


def gather_kernel(source_ref, rows_ref, out_ref):
    def body(block, carry):
        first = pl.multiple_of(block * 128, 128)
        parts = [rows_ref[pl.ds(source_ref[first + k], 1), :] for k in range(128)]
        out_ref[:, pl.ds(first, 128)] = jnp.concatenate(parts, axis=0).T
        return carry

    lax.fori_loop(0, out_ref.shape[1] // 128, body, 0, unroll=2)


def scatter_rows(target, columns, slots):
    return pl.pallas_call(
        scatter_kernel,
        out_shape=jax.ShapeDtypeStruct((slots, columns.shape[0]), columns.dtype),
        in_specs=[pl.BlockSpec(memory_space=pltpu.SMEM), pl.BlockSpec(memory_space=pltpu.VMEM)],
        out_specs=pl.BlockSpec(memory_space=pltpu.VMEM),
    )(target, columns)


def gather_rows(source, rows):
    return pl.pallas_call(
        gather_kernel,
        out_shape=jax.ShapeDtypeStruct((rows.shape[1], source.shape[0]), rows.dtype),
        in_specs=[pl.BlockSpec(memory_space=pltpu.SMEM), pl.BlockSpec(memory_space=pltpu.VMEM)],
        out_specs=pl.BlockSpec(memory_space=pltpu.VMEM),
    )(source, rows)


def flat_chunks(rows, devices):
    slots, width = rows.shape
    chunk = slots // devices * width
    padded = -(-chunk // 1024) * 1024
    flat = jnp.pad(rows.reshape(devices, chunk), ((0, 0), (0, padded - chunk)))
    return flat.reshape(devices, padded // 128, 128)


def exchange_chunks(flat, slots, width):
    devices = flat.shape[0]
    chunk = slots // devices * width
    arrived = lax.all_to_all(flat, ("band", "lon"), 0, 0, tiled=True)
    return arrived.reshape(devices, -1)[:, :chunk].reshape(slots, width)


def slot_of(tiles, devices, block_rows):
    count = tiles.shape[0]
    blocks = count // block_rows
    one_hot = (tiles[:, None] == jnp.arange(devices, dtype=jnp.int32)[None, :]).astype(jnp.bfloat16)
    one_hot = one_hot.reshape(blocks, block_rows, devices)
    positions = jnp.arange(block_rows, dtype=jnp.int32)
    lower_tri = (positions[:, None] > positions[None, :]).astype(jnp.bfloat16)
    within = jnp.einsum("ab,kbt->kat", lower_tri, one_hot, preferred_element_type=jnp.float32)
    totals = jnp.sum(one_hot.astype(jnp.float32), axis=1)
    offsets = jnp.cumsum(totals, axis=0) - totals
    before = within + offsets[:, None, :]
    rank = jnp.sum(before * one_hot.astype(jnp.float32), axis=2)
    return rank.reshape(count).astype(jnp.int32)


def on_device(
    control,
    background_std,
    diffusivity,
    land_sea,
    departures,
    obs_frac,
    obs_weight,
    obs_cell,
    obs_tile,
):
    values = control.shape[0]
    tile_lat = control.shape[1]
    tile_lon = control.shape[2]
    band_count = lax.axis_size("band")
    lon_count = lax.axis_size("lon")
    devices = band_count * lon_count
    count = obs_tile.shape[0]
    block_rows = 512
    blocks = count // block_rows
    capacity = 5 * count // (4 * devices)
    slots = devices * capacity
    tiles = obs_tile[:, 0]
    target = tiles * capacity + slot_of(tiles, devices, block_rows)
    target = jnp.clip(target, 0, slots - 1)
    payload = jnp.concatenate(
        [departures, obs_frac, obs_weight[None, :], obs_cell.astype(jnp.float32)[None, :]], axis=0
    )
    outgoing = flat_chunks(scatter_rows(target, payload, slots), devices)
    outgoing, control, diffusivity, land_sea = lax.optimization_barrier(
        (outgoing, control, diffusivity, land_sea)
    )
    sea = land_sea.astype(jnp.float32)
    depth = PASSES
    stacked = jnp.concatenate([control * sea[None], diffusivity[None], sea[None]], axis=0)
    rimmed = with_halo(stacked, depth)
    lat_rows = (
        lax.axis_index("band") * tile_lat
        - depth
        + jnp.arange(tile_lat + 2 * depth, dtype=jnp.int32)
    )
    inside = ((lat_rows >= 0) & (lat_rows < band_count * tile_lat)).astype(jnp.float32)
    south, east = face_weights(rimmed[values], rimmed[values + 1] * inside[:, None])
    state = smooth_padded(rimmed[:values], south, east)
    increment = state * background_std[:, None, None]
    arrived = exchange_chunks(outgoing, slots, values + 4).T
    depart = arrived[:values]
    lat_frac = arrived[values]
    lon_frac = arrived[values + 1]
    row_weight = arrived[values + 2]
    cell = arrived[values + 3].astype(jnp.int32)
    lat_start = cell // (tile_lon - 1)
    lon_start = cell % (tile_lon - 1)
    lat_ids = jnp.arange(tile_lat, dtype=jnp.int32)[:, None]
    lon_ids = jnp.arange(tile_lon, dtype=jnp.int32)[:, None]
    lat_table = (lat_ids == lat_start[None, :]).astype(jnp.float32) * (1.0 - lat_frac)[None, :]
    lat_table = (
        lat_table + (lat_ids == lat_start[None, :] + 1).astype(jnp.float32) * lat_frac[None, :]
    )
    lon_table = (lon_ids == lon_start[None, :]).astype(jnp.float32) * (1.0 - lon_frac)[None, :]
    lon_table = (
        lon_table + (lon_ids == lon_start[None, :] + 1).astype(jnp.float32) * lon_frac[None, :]
    )
    partial_rows = jnp.einsum(
        "vij,jn->vin", increment, lon_table, precision=HIGH, preferred_element_type=jnp.float32
    )
    equiv = jnp.sum(partial_rows * lat_table[None, :, :], axis=1)
    misfit = row_weight * (equiv - depart)
    back = flat_chunks(misfit.T, devices)
    back, misfit = lax.optimization_barrier((back, misfit))
    spread = misfit[:, None, :] * lat_table[None, :, :]
    adjoint = jnp.einsum(
        "vin,jn->vij", spread, lon_table, precision=HIGH, preferred_element_type=jnp.float32
    )
    adjoint = adjoint * background_std[:, None, None]
    gradient = control + sea[None] * smooth(adjoint, south, east)
    returned = exchange_chunks(back, slots, values)
    obs_residual = gather_rows(target, returned)
    return (gradient, obs_residual)


def solution(mesh):
    in_specs = (
        P(None, "band", "lon"),
        P(),
        P("band", "lon"),
        P("band", "lon"),
        P(None, ("band", "lon")),
        P(None, ("band", "lon")),
        P(("band", "lon")),
        P(("band", "lon")),
        P(("band", "lon"), None),
    )
    out_specs = (P(None, "band", "lon"), P(None, ("band", "lon")))
    return jax.shard_map(
        on_device, mesh=mesh, in_specs=in_specs, out_specs=out_specs, check_vma=False
    )
```

```python
import jax
import jax.numpy as jnp
from jax import lax
from jax.experimental import pallas as pl
from jax.experimental.pallas import tpu as pltpu
from jax.sharding import PartitionSpec as P

PASSES = 4


HIGH = lax.Precision.HIGH


def ring_halo(array, axis, dim, width):
    count, length = (lax.axis_size(axis), array.shape[dim])
    up = [(i, (i + 1) % count) for i in range(count)]
    down = [(j, i) for i, j in up]
    last = lax.slice_in_dim(array, length - width, length, axis=dim)
    initial = lax.slice_in_dim(array, 0, width, axis=dim)
    before = lax.ppermute(last, axis, up)
    after = lax.ppermute(initial, axis, down)
    return jnp.concatenate([before, array, after], axis=dim)


def with_halo(array, width):
    array = ring_halo(array, "band", array.ndim - 2, width)
    return ring_halo(array, "lon", array.ndim - 1, width)


def face_weights(kappa_pad, sea_pad):
    south = 0.5 * (kappa_pad[:-1, :] + kappa_pad[1:, :]) * sea_pad[:-1, :] * sea_pad[1:, :]
    east = 0.5 * (kappa_pad[:, :-1] + kappa_pad[:, 1:]) * sea_pad[:, :-1] * sea_pad[:, 1:]
    return (south, east)


def diffuse_once(field, south, east):
    flux_south = south * (field[:, 1:, :] - field[:, :-1, :])
    flux_east = east * (field[:, :, 1:] - field[:, :, :-1])
    zero_lat = ((0, 0), (0, 1), (0, 0))
    along_lat = jnp.pad(flux_south, zero_lat) - jnp.pad(flux_south, ((0, 0), (1, 0), (0, 0)))
    along_lon = jnp.pad(flux_east, ((0, 0), (0, 0), (0, 1))) - jnp.pad(flux_east, ((0, 0), (0, 0), (1, 0)))
    return field + along_lat + along_lon


def smooth_padded(result, south, east):
    tile_lat, tile_lon = result.shape[1] - 2 * PASSES, result.shape[2] - 2 * PASSES
    result = lax.fori_loop(0, PASSES, lambda step, field: diffuse_once(field, south, east), result)
    return result[:, PASSES:PASSES + tile_lat, PASSES:PASSES + tile_lon]


def smooth(field, south, east):
    return smooth_padded(with_halo(field, PASSES), south, east)


def scatter_kernel(target_ref, columns_ref, out_ref):
    out_ref[...] = jnp.zeros(out_ref.shape, out_ref.dtype)

    def body(block, carry):
        first = pl.multiple_of(block * 128, 128)
        rows = columns_ref[:, pl.ds(first, 128)].T
        for k in range(128):
            out_ref[pl.ds(target_ref[first + k], 1), :] = rows[k:k + 1, :]
        return carry

    lax.fori_loop(0, columns_ref.shape[1] // 128, body, 0, unroll=4)


def gather_kernel(source_ref, rows_ref, out_ref):
    def body(block, carry):
        first = pl.multiple_of(block * 128, 128)
        parts = [rows_ref[pl.ds(source_ref[first + k], 1), :] for k in range(128)]
        out_ref[:, pl.ds(first, 128)] = jnp.concatenate(parts, axis=0).T
        return carry

    lax.fori_loop(0, out_ref.shape[1] // 128, body, 0, unroll=4)


def scatter_rows(target, columns, slots):
    return pl.pallas_call(
        scatter_kernel,
        out_shape=jax.ShapeDtypeStruct((slots, columns.shape[0]), columns.dtype),
        in_specs=[pl.BlockSpec(memory_space=pltpu.SMEM), pl.BlockSpec(memory_space=pltpu.VMEM)],
        out_specs=pl.BlockSpec(memory_space=pltpu.VMEM),
    )(target, columns)


def gather_rows(source, rows):
    return pl.pallas_call(
        gather_kernel,
        out_shape=jax.ShapeDtypeStruct((rows.shape[1], source.shape[0]), rows.dtype),
        in_specs=[pl.BlockSpec(memory_space=pltpu.SMEM), pl.BlockSpec(memory_space=pltpu.VMEM)],
        out_specs=pl.BlockSpec(memory_space=pltpu.VMEM),
    )(source, rows)


def flat_chunks(rows, devices):
    slots, width = rows.shape
    chunk = slots // devices * width
    padded = -(-chunk // 1024) * 1024
    flat = jnp.pad(rows.reshape(devices, chunk), ((0, 0), (0, padded - chunk)))
    return flat.reshape(devices, padded // 128, 128)


def exchange_chunks(flat, slots, width):
    devices = flat.shape[0]
    chunk = slots // devices * width
    arrived = lax.all_to_all(flat, ("band", "lon"), 0, 0, tiled=True)
    return arrived.reshape(devices, -1)[:, :chunk].reshape(slots, width)


def slot_of(tiles, devices, block_rows):
    count = tiles.shape[0]
    blocks = count // block_rows
    one_hot = (tiles[:, None] == jnp.arange(devices, dtype=jnp.int32)[None, :]).astype(jnp.bfloat16)
    one_hot = one_hot.reshape(blocks, block_rows, devices)
    positions = jnp.arange(block_rows, dtype=jnp.int32)
    lower_tri = (positions[:, None] > positions[None, :]).astype(jnp.bfloat16)
    within = jnp.einsum("ab,kbt->kat", lower_tri, one_hot, preferred_element_type=jnp.float32)
    totals = jnp.sum(one_hot.astype(jnp.float32), axis=1)
    offsets = jnp.cumsum(totals, axis=0) - totals
    before = within + offsets[:, None, :]
    rank = jnp.sum(before * one_hot.astype(jnp.float32), axis=2)
    return rank.reshape(count).astype(jnp.int32)


def on_device(
    control,
    background_std,
    diffusivity,
    land_sea,
    departures,
    obs_frac,
    obs_weight,
    obs_cell,
    obs_tile,
):
    values = control.shape[0]
    tile_lat = control.shape[1]
    tile_lon = control.shape[2]
    band_count = lax.axis_size("band")
    lon_count = lax.axis_size("lon")
    devices = band_count * lon_count
    count = obs_tile.shape[0]
    block_rows = 512
    blocks = count // block_rows
    capacity = 5 * count // (4 * devices)
    slots = devices * capacity
    tiles = obs_tile[:, 0]
    target = tiles * capacity + slot_of(tiles, devices, block_rows)
    target = jnp.clip(target, 0, slots - 1)
    payload = jnp.concatenate(
        [departures, obs_frac, obs_weight[None, :], obs_cell.astype(jnp.float32)[None, :]], axis=0
    )
    outgoing = flat_chunks(scatter_rows(target, payload, slots), devices)
    outgoing, control, diffusivity, land_sea = lax.optimization_barrier(
        (outgoing, control, diffusivity, land_sea)
    )
    sea = land_sea.astype(jnp.float32)
    depth = PASSES
    stacked = jnp.concatenate([control * sea[None], diffusivity[None], sea[None]], axis=0)
    rimmed = with_halo(stacked, depth)
    lat_rows = (
        lax.axis_index("band") * tile_lat
        - depth
        + jnp.arange(tile_lat + 2 * depth, dtype=jnp.int32)
    )
    inside = ((lat_rows >= 0) & (lat_rows < band_count * tile_lat)).astype(jnp.float32)
    south, east = face_weights(rimmed[values], rimmed[values + 1] * inside[:, None])
    state = smooth_padded(rimmed[:values], south, east)
    increment = state * background_std[:, None, None]
    arrived = exchange_chunks(outgoing, slots, values + 4).T
    depart = arrived[:values]
    lat_frac = arrived[values]
    lon_frac = arrived[values + 1]
    row_weight = arrived[values + 2]
    cell = arrived[values + 3].astype(jnp.int32)
    lat_start = cell // (tile_lon - 1)
    lon_start = cell % (tile_lon - 1)
    lat_ids = jnp.arange(tile_lat, dtype=jnp.int32)[:, None]
    lon_ids = jnp.arange(tile_lon, dtype=jnp.int32)[:, None]
    lat_table = (lat_ids == lat_start[None, :]).astype(jnp.float32) * (1.0 - lat_frac)[None, :]
    lat_table = (
        lat_table + (lat_ids == lat_start[None, :] + 1).astype(jnp.float32) * lat_frac[None, :]
    )
    lon_table = (lon_ids == lon_start[None, :]).astype(jnp.float32) * (1.0 - lon_frac)[None, :]
    lon_table = (
        lon_table + (lon_ids == lon_start[None, :] + 1).astype(jnp.float32) * lon_frac[None, :]
    )
    partial_rows = jnp.einsum(
        "vij,jn->vin", increment, lon_table, precision=HIGH, preferred_element_type=jnp.float32
    )
    equiv = jnp.sum(partial_rows * lat_table[None, :, :], axis=1)
    misfit = row_weight * (equiv - depart)
    back = flat_chunks(misfit.T, devices)
    back, misfit = lax.optimization_barrier((back, misfit))
    spread = misfit[:, None, :] * lat_table[None, :, :]
    adjoint = jnp.einsum(
        "vin,jn->vij", spread, lon_table, precision=HIGH, preferred_element_type=jnp.float32
    )
    adjoint = adjoint * background_std[:, None, None]
    gradient = control + sea[None] * smooth(adjoint, south, east)
    returned = exchange_chunks(back, slots, values)
    obs_residual = gather_rows(target, returned)
    return (gradient, obs_residual)


def solution(mesh):
    in_specs = (
        P(None, "band", "lon"),
        P(),
        P("band", "lon"),
        P("band", "lon"),
        P(None, ("band", "lon")),
        P(None, ("band", "lon")),
        P(("band", "lon")),
        P(("band", "lon")),
        P(("band", "lon"), None),
    )
    out_specs = (P(None, "band", "lon"), P(None, ("band", "lon")))
    return jax.shard_map(
        on_device, mesh=mesh, in_specs=in_specs, out_specs=out_specs, check_vma=False
    )
```

```python
import jax
import jax.numpy as jnp
from jax import lax
from jax.experimental import pallas as pl
from jax.experimental.pallas import tpu as pltpu
from jax.sharding import PartitionSpec as P

PASSES = 4


HIGH = lax.Precision.HIGH


def ring_halo(array, axis, dim, width):
    count, length = (lax.axis_size(axis), array.shape[dim])
    up = [(i, (i + 1) % count) for i in range(count)]
    down = [(j, i) for i, j in up]
    last = lax.slice_in_dim(array, length - width, length, axis=dim)
    initial = lax.slice_in_dim(array, 0, width, axis=dim)
    before = lax.ppermute(last, axis, up)
    after = lax.ppermute(initial, axis, down)
    return jnp.concatenate([before, array, after], axis=dim)


def with_halo(array, width):
    array = ring_halo(array, "band", array.ndim - 2, width)
    return ring_halo(array, "lon", array.ndim - 1, width)


def face_weights(kappa_pad, sea_pad):
    south = 0.5 * (kappa_pad[:-1, :] + kappa_pad[1:, :]) * sea_pad[:-1, :] * sea_pad[1:, :]
    east = 0.5 * (kappa_pad[:, :-1] + kappa_pad[:, 1:]) * sea_pad[:, :-1] * sea_pad[:, 1:]
    return (south, east)


def diffuse_once(field, south, east):
    flux_south = south * (field[:, 1:, :] - field[:, :-1, :])
    flux_east = east * (field[:, :, 1:] - field[:, :, :-1])
    zero_lat = ((0, 0), (0, 1), (0, 0))
    along_lat = jnp.pad(flux_south, zero_lat) - jnp.pad(flux_south, ((0, 0), (1, 0), (0, 0)))
    along_lon = jnp.pad(flux_east, ((0, 0), (0, 0), (0, 1))) - jnp.pad(flux_east, ((0, 0), (0, 0), (1, 0)))
    return field + along_lat + along_lon


def smooth_padded(result, south, east):
    tile_lat, tile_lon = result.shape[1] - 2 * PASSES, result.shape[2] - 2 * PASSES
    result = lax.fori_loop(0, PASSES, lambda step, field: diffuse_once(field, south, east), result)
    return result[:, PASSES:PASSES + tile_lat, PASSES:PASSES + tile_lon]


def smooth(field, south, east):
    return smooth_padded(with_halo(field, PASSES), south, east)


def scatter_kernel(target_ref, columns_ref, out_ref):
    out_ref[...] = jnp.zeros(out_ref.shape, out_ref.dtype)

    def body(block, carry):
        first = pl.multiple_of(block * 128, 128)
        rows = columns_ref[:, pl.ds(first, 128)].T
        for k in range(128):
            out_ref[pl.ds(target_ref[first + k], 1), :] = rows[k:k + 1, :]
        return carry

    lax.fori_loop(0, columns_ref.shape[1] // 128, body, 0, unroll=8)


def gather_kernel(source_ref, rows_ref, out_ref):
    def body(block, carry):
        first = pl.multiple_of(block * 128, 128)
        parts = [rows_ref[pl.ds(source_ref[first + k], 1), :] for k in range(128)]
        out_ref[:, pl.ds(first, 128)] = jnp.concatenate(parts, axis=0).T
        return carry

    lax.fori_loop(0, out_ref.shape[1] // 128, body, 0, unroll=8)


def scatter_rows(target, columns, slots):
    return pl.pallas_call(
        scatter_kernel,
        out_shape=jax.ShapeDtypeStruct((slots, columns.shape[0]), columns.dtype),
        in_specs=[pl.BlockSpec(memory_space=pltpu.SMEM), pl.BlockSpec(memory_space=pltpu.VMEM)],
        out_specs=pl.BlockSpec(memory_space=pltpu.VMEM),
    )(target, columns)


def gather_rows(source, rows):
    return pl.pallas_call(
        gather_kernel,
        out_shape=jax.ShapeDtypeStruct((rows.shape[1], source.shape[0]), rows.dtype),
        in_specs=[pl.BlockSpec(memory_space=pltpu.SMEM), pl.BlockSpec(memory_space=pltpu.VMEM)],
        out_specs=pl.BlockSpec(memory_space=pltpu.VMEM),
    )(source, rows)


def flat_chunks(rows, devices):
    slots, width = rows.shape
    chunk = slots // devices * width
    padded = -(-chunk // 1024) * 1024
    flat = jnp.pad(rows.reshape(devices, chunk), ((0, 0), (0, padded - chunk)))
    return flat.reshape(devices, padded // 128, 128)


def exchange_chunks(flat, slots, width):
    devices = flat.shape[0]
    chunk = slots // devices * width
    arrived = lax.all_to_all(flat, ("band", "lon"), 0, 0, tiled=True)
    return arrived.reshape(devices, -1)[:, :chunk].reshape(slots, width)


def slot_of(tiles, devices, block_rows):
    count = tiles.shape[0]
    blocks = count // block_rows
    one_hot = (tiles[:, None] == jnp.arange(devices, dtype=jnp.int32)[None, :]).astype(jnp.bfloat16)
    one_hot = one_hot.reshape(blocks, block_rows, devices)
    positions = jnp.arange(block_rows, dtype=jnp.int32)
    lower_tri = (positions[:, None] > positions[None, :]).astype(jnp.bfloat16)
    within = jnp.einsum("ab,kbt->kat", lower_tri, one_hot, preferred_element_type=jnp.float32)
    totals = jnp.sum(one_hot.astype(jnp.float32), axis=1)
    offsets = jnp.cumsum(totals, axis=0) - totals
    before = within + offsets[:, None, :]
    rank = jnp.sum(before * one_hot.astype(jnp.float32), axis=2)
    return rank.reshape(count).astype(jnp.int32)


def on_device(
    control,
    background_std,
    diffusivity,
    land_sea,
    departures,
    obs_frac,
    obs_weight,
    obs_cell,
    obs_tile,
):
    values = control.shape[0]
    tile_lat = control.shape[1]
    tile_lon = control.shape[2]
    band_count = lax.axis_size("band")
    lon_count = lax.axis_size("lon")
    devices = band_count * lon_count
    count = obs_tile.shape[0]
    block_rows = 512
    blocks = count // block_rows
    capacity = 5 * count // (4 * devices)
    slots = devices * capacity
    tiles = obs_tile[:, 0]
    target = tiles * capacity + slot_of(tiles, devices, block_rows)
    target = jnp.clip(target, 0, slots - 1)
    payload = jnp.concatenate(
        [departures, obs_frac, obs_weight[None, :], obs_cell.astype(jnp.float32)[None, :]], axis=0
    )
    outgoing = flat_chunks(scatter_rows(target, payload, slots), devices)
    outgoing, control, diffusivity, land_sea = lax.optimization_barrier(
        (outgoing, control, diffusivity, land_sea)
    )
    sea = land_sea.astype(jnp.float32)
    depth = PASSES
    stacked = jnp.concatenate([control * sea[None], diffusivity[None], sea[None]], axis=0)
    rimmed = with_halo(stacked, depth)
    lat_rows = (
        lax.axis_index("band") * tile_lat
        - depth
        + jnp.arange(tile_lat + 2 * depth, dtype=jnp.int32)
    )
    inside = ((lat_rows >= 0) & (lat_rows < band_count * tile_lat)).astype(jnp.float32)
    south, east = face_weights(rimmed[values], rimmed[values + 1] * inside[:, None])
    state = smooth_padded(rimmed[:values], south, east)
    increment = state * background_std[:, None, None]
    arrived = exchange_chunks(outgoing, slots, values + 4).T
    depart = arrived[:values]
    lat_frac = arrived[values]
    lon_frac = arrived[values + 1]
    row_weight = arrived[values + 2]
    cell = arrived[values + 3].astype(jnp.int32)
    lat_start = cell // (tile_lon - 1)
    lon_start = cell % (tile_lon - 1)
    lat_ids = jnp.arange(tile_lat, dtype=jnp.int32)[:, None]
    lon_ids = jnp.arange(tile_lon, dtype=jnp.int32)[:, None]
    lat_table = (lat_ids == lat_start[None, :]).astype(jnp.float32) * (1.0 - lat_frac)[None, :]
    lat_table = (
        lat_table + (lat_ids == lat_start[None, :] + 1).astype(jnp.float32) * lat_frac[None, :]
    )
    lon_table = (lon_ids == lon_start[None, :]).astype(jnp.float32) * (1.0 - lon_frac)[None, :]
    lon_table = (
        lon_table + (lon_ids == lon_start[None, :] + 1).astype(jnp.float32) * lon_frac[None, :]
    )
    partial_rows = jnp.einsum(
        "vij,jn->vin", increment, lon_table, precision=HIGH, preferred_element_type=jnp.float32
    )
    equiv = jnp.sum(partial_rows * lat_table[None, :, :], axis=1)
    misfit = row_weight * (equiv - depart)
    back = flat_chunks(misfit.T, devices)
    back, misfit = lax.optimization_barrier((back, misfit))
    spread = misfit[:, None, :] * lat_table[None, :, :]
    adjoint = jnp.einsum(
        "vin,jn->vij", spread, lon_table, precision=HIGH, preferred_element_type=jnp.float32
    )
    adjoint = adjoint * background_std[:, None, None]
    gradient = control + sea[None] * smooth(adjoint, south, east)
    returned = exchange_chunks(back, slots, values)
    obs_residual = gather_rows(target, returned)
    return (gradient, obs_residual)


def solution(mesh):
    in_specs = (
        P(None, "band", "lon"),
        P(),
        P("band", "lon"),
        P("band", "lon"),
        P(None, ("band", "lon")),
        P(None, ("band", "lon")),
        P(("band", "lon")),
        P(("band", "lon")),
        P(("band", "lon"), None),
    )
    out_specs = (P(None, "band", "lon"), P(None, ("band", "lon")))
    return jax.shard_map(
        on_device, mesh=mesh, in_specs=in_specs, out_specs=out_specs, check_vma=False
    )
```

```python
import jax
import jax.numpy as jnp
from jax import lax
from jax.experimental import pallas as pl
from jax.experimental.pallas import tpu as pltpu
from jax.sharding import PartitionSpec as P

PASSES = 4


HIGH = lax.Precision.HIGH


def ring_halo(array, axis, dim, width):
    count, length = (lax.axis_size(axis), array.shape[dim])
    up = [(i, (i + 1) % count) for i in range(count)]
    down = [(j, i) for i, j in up]
    last = lax.slice_in_dim(array, length - width, length, axis=dim)
    initial = lax.slice_in_dim(array, 0, width, axis=dim)
    before = lax.ppermute(last, axis, up)
    after = lax.ppermute(initial, axis, down)
    return jnp.concatenate([before, array, after], axis=dim)


def with_halo(array, width):
    array = ring_halo(array, "band", array.ndim - 2, width)
    return ring_halo(array, "lon", array.ndim - 1, width)


def face_weights(kappa_pad, sea_pad):
    south = 0.5 * (kappa_pad[:-1, :] + kappa_pad[1:, :]) * sea_pad[:-1, :] * sea_pad[1:, :]
    east = 0.5 * (kappa_pad[:, :-1] + kappa_pad[:, 1:]) * sea_pad[:, :-1] * sea_pad[:, 1:]
    return (south, east)


def diffuse_once(field, south, east):
    flux_south = south * (field[:, 1:, :] - field[:, :-1, :])
    flux_east = east * (field[:, :, 1:] - field[:, :, :-1])
    zero_lat = ((0, 0), (0, 1), (0, 0))
    along_lat = jnp.pad(flux_south, zero_lat) - jnp.pad(flux_south, ((0, 0), (1, 0), (0, 0)))
    along_lon = jnp.pad(flux_east, ((0, 0), (0, 0), (0, 1))) - jnp.pad(flux_east, ((0, 0), (0, 0), (1, 0)))
    return field + along_lat + along_lon


def smooth_padded(result, south, east):
    tile_lat, tile_lon = result.shape[1] - 2 * PASSES, result.shape[2] - 2 * PASSES
    result = lax.fori_loop(0, PASSES, lambda step, field: diffuse_once(field, south, east), result)
    return result[:, PASSES:PASSES + tile_lat, PASSES:PASSES + tile_lon]


def smooth(field, south, east):
    return smooth_padded(with_halo(field, PASSES), south, east)


def scatter_kernel(target_ref, columns_ref, out_ref):
    out_ref[...] = jnp.zeros(out_ref.shape, out_ref.dtype)

    def body(block, carry):
        first = pl.multiple_of(block * 128, 128)
        rows = columns_ref[:, pl.ds(first, 128)].T
        for k in range(128):
            out_ref[pl.ds(target_ref[first + k], 1), :] = rows[k:k + 1, :]
        return carry

    lax.fori_loop(0, columns_ref.shape[1] // 128, body, 0, unroll=16)


def gather_kernel(source_ref, rows_ref, out_ref):
    def body(block, carry):
        first = pl.multiple_of(block * 128, 128)
        parts = [rows_ref[pl.ds(source_ref[first + k], 1), :] for k in range(128)]
        out_ref[:, pl.ds(first, 128)] = jnp.concatenate(parts, axis=0).T
        return carry

    lax.fori_loop(0, out_ref.shape[1] // 128, body, 0, unroll=16)


def scatter_rows(target, columns, slots):
    return pl.pallas_call(
        scatter_kernel,
        out_shape=jax.ShapeDtypeStruct((slots, columns.shape[0]), columns.dtype),
        in_specs=[pl.BlockSpec(memory_space=pltpu.SMEM), pl.BlockSpec(memory_space=pltpu.VMEM)],
        out_specs=pl.BlockSpec(memory_space=pltpu.VMEM),
    )(target, columns)


def gather_rows(source, rows):
    return pl.pallas_call(
        gather_kernel,
        out_shape=jax.ShapeDtypeStruct((rows.shape[1], source.shape[0]), rows.dtype),
        in_specs=[pl.BlockSpec(memory_space=pltpu.SMEM), pl.BlockSpec(memory_space=pltpu.VMEM)],
        out_specs=pl.BlockSpec(memory_space=pltpu.VMEM),
    )(source, rows)


def flat_chunks(rows, devices):
    slots, width = rows.shape
    chunk = slots // devices * width
    padded = -(-chunk // 1024) * 1024
    flat = jnp.pad(rows.reshape(devices, chunk), ((0, 0), (0, padded - chunk)))
    return flat.reshape(devices, padded // 128, 128)


def exchange_chunks(flat, slots, width):
    devices = flat.shape[0]
    chunk = slots // devices * width
    arrived = lax.all_to_all(flat, ("band", "lon"), 0, 0, tiled=True)
    return arrived.reshape(devices, -1)[:, :chunk].reshape(slots, width)


def slot_of(tiles, devices, block_rows):
    count = tiles.shape[0]
    blocks = count // block_rows
    one_hot = (tiles[:, None] == jnp.arange(devices, dtype=jnp.int32)[None, :]).astype(jnp.bfloat16)
    one_hot = one_hot.reshape(blocks, block_rows, devices)
    positions = jnp.arange(block_rows, dtype=jnp.int32)
    lower_tri = (positions[:, None] > positions[None, :]).astype(jnp.bfloat16)
    within = jnp.einsum("ab,kbt->kat", lower_tri, one_hot, preferred_element_type=jnp.float32)
    totals = jnp.sum(one_hot.astype(jnp.float32), axis=1)
    offsets = jnp.cumsum(totals, axis=0) - totals
    before = within + offsets[:, None, :]
    rank = jnp.sum(before * one_hot.astype(jnp.float32), axis=2)
    return rank.reshape(count).astype(jnp.int32)


def on_device(
    control,
    background_std,
    diffusivity,
    land_sea,
    departures,
    obs_frac,
    obs_weight,
    obs_cell,
    obs_tile,
):
    values = control.shape[0]
    tile_lat = control.shape[1]
    tile_lon = control.shape[2]
    band_count = lax.axis_size("band")
    lon_count = lax.axis_size("lon")
    devices = band_count * lon_count
    count = obs_tile.shape[0]
    block_rows = 512
    blocks = count // block_rows
    capacity = 5 * count // (4 * devices)
    slots = devices * capacity
    tiles = obs_tile[:, 0]
    target = tiles * capacity + slot_of(tiles, devices, block_rows)
    target = jnp.clip(target, 0, slots - 1)
    payload = jnp.concatenate(
        [departures, obs_frac, obs_weight[None, :], obs_cell.astype(jnp.float32)[None, :]], axis=0
    )
    outgoing = flat_chunks(scatter_rows(target, payload, slots), devices)
    outgoing, control, diffusivity, land_sea = lax.optimization_barrier(
        (outgoing, control, diffusivity, land_sea)
    )
    sea = land_sea.astype(jnp.float32)
    depth = PASSES
    stacked = jnp.concatenate([control * sea[None], diffusivity[None], sea[None]], axis=0)
    rimmed = with_halo(stacked, depth)
    lat_rows = (
        lax.axis_index("band") * tile_lat
        - depth
        + jnp.arange(tile_lat + 2 * depth, dtype=jnp.int32)
    )
    inside = ((lat_rows >= 0) & (lat_rows < band_count * tile_lat)).astype(jnp.float32)
    south, east = face_weights(rimmed[values], rimmed[values + 1] * inside[:, None])
    state = smooth_padded(rimmed[:values], south, east)
    increment = state * background_std[:, None, None]
    arrived = exchange_chunks(outgoing, slots, values + 4).T
    depart = arrived[:values]
    lat_frac = arrived[values]
    lon_frac = arrived[values + 1]
    row_weight = arrived[values + 2]
    cell = arrived[values + 3].astype(jnp.int32)
    lat_start = cell // (tile_lon - 1)
    lon_start = cell % (tile_lon - 1)
    lat_ids = jnp.arange(tile_lat, dtype=jnp.int32)[:, None]
    lon_ids = jnp.arange(tile_lon, dtype=jnp.int32)[:, None]
    lat_table = (lat_ids == lat_start[None, :]).astype(jnp.float32) * (1.0 - lat_frac)[None, :]
    lat_table = (
        lat_table + (lat_ids == lat_start[None, :] + 1).astype(jnp.float32) * lat_frac[None, :]
    )
    lon_table = (lon_ids == lon_start[None, :]).astype(jnp.float32) * (1.0 - lon_frac)[None, :]
    lon_table = (
        lon_table + (lon_ids == lon_start[None, :] + 1).astype(jnp.float32) * lon_frac[None, :]
    )
    partial_rows = jnp.einsum(
        "vij,jn->vin", increment, lon_table, precision=HIGH, preferred_element_type=jnp.float32
    )
    equiv = jnp.sum(partial_rows * lat_table[None, :, :], axis=1)
    misfit = row_weight * (equiv - depart)
    back = flat_chunks(misfit.T, devices)
    back, misfit = lax.optimization_barrier((back, misfit))
    spread = misfit[:, None, :] * lat_table[None, :, :]
    adjoint = jnp.einsum(
        "vin,jn->vij", spread, lon_table, precision=HIGH, preferred_element_type=jnp.float32
    )
    adjoint = adjoint * background_std[:, None, None]
    gradient = control + sea[None] * smooth(adjoint, south, east)
    returned = exchange_chunks(back, slots, values)
    obs_residual = gather_rows(target, returned)
    return (gradient, obs_residual)


def solution(mesh):
    in_specs = (
        P(None, "band", "lon"),
        P(),
        P("band", "lon"),
        P("band", "lon"),
        P(None, ("band", "lon")),
        P(None, ("band", "lon")),
        P(("band", "lon")),
        P(("band", "lon")),
        P(("band", "lon"), None),
    )
    out_specs = (P(None, "band", "lon"), P(None, ("band", "lon")))
    return jax.shard_map(
        on_device, mesh=mesh, in_specs=in_specs, out_specs=out_specs, check_vma=False
    )
```
